512 devices in a mesh: gx: 8 (over z), gy: 8 (over y), gz: 8 (over x, core).
Axes of the slice: x: 4, y: 8, z: 8, core: 2. Of those that a mesh axis runs over, the one named last changes fastest.
Arguments:
- state: bfloat16 [5, 32, 64, 6144], P(None, 'gx', 'gy', 'gz'), may hold values from -6 to 6
- diffusivity: bfloat16 [32, 64, 6144], P('gx', 'gy', 'gz'), may hold values from 0.25 to 1
- coupling: float32 [5, 5], replicated, may hold values from -3 to 3
- owner: int32 [24576, 1], P(('gx', 'gy', 'gz')), may hold values from 0 to 63; in each aligned block of 48 rows (0 to 47, 48 to 95, ...) at most 2 rows name the same one
- levels: int32 [24576], P(('gx', 'gy', 'gz')), may hold values from 0 to 3
- mark_count: int32 [1], replicated, may hold values from 12288 to 24575
- goal_weight: bfloat16 [65536, 5, 2, 2, 128], P(('gx', 'gy', 'gz')), may hold values from -6 to 6
- reaction: bfloat16 [65536, 5], P(('gx', 'gy', 'gz')), may hold values from 0.5 to 2
Outputs:
- adjoint_field: bfloat16 [5, 32, 64, 6144], P(None, 'gx', 'gy', 'gz')
- share: float32 [24576], P(('gx', 'gy', 'gz'))
- marked: float32 [24576], P(('gx', 'gy', 'gz'))
The draws below stay inside these ranges and needn't reach their ends.
Inputs may be any that keep to these rules, and one draw needn't show every extreme that they name: owner names a device among the 64 that share the block's gx index (in the order gy, gz); no more than 2 blocks of one device name the same owner.
All inputs are finite; a program needn't handle non-finite values.
Results may differ from the reference program's by a relative error of at most 0.0031.
Values may be sent and summed in bfloat16 or wider, within the bound.
No kernel may reach another device: no remote copies, remote signals or barrier semaphores. Data moves between devices by JAX's collectives and lax.ppermute only.
A program may use at most 64 MiB of HBM per device.

```python
import math
import jax
import jax.numpy as jnp
import numpy as np
from jax import lax

FIELDS = 5
BX = 2
BY = 2
BZ = 128
NBX = 2
NBY = 4
NBZ = 6
SECTIONS = 3
BLK_DEV = 48
PLANE = 64
SLOT_CAP = 2
BLOCKS = 24576
SLOTS = 65536
NX = 32
NY = 64
NZ = 6144
N_GX = 8
N_GY = 8
N_GZ = 8
DEVICES = 512


def place_ends(drawn, key, least, top_value):
    index_at = [jax.random.randint(jax.random.fold_in(key, axis), (), 0, length) for axis, length in enumerate(drawn.shape)]
    widest = drawn.shape.index(max(drawn.shape))
    neighbour = index_at[:widest] + [(index_at[widest] + 1) % drawn.shape[widest]] + index_at[widest + 1:]
    return drawn.at[tuple(index_at)].set(least).at[tuple(neighbour)].set(top_value)


def level_of(own_key, extent, shards, smallest, high):
    gain = 1.0
    for dim, blocks in shards:
        heights = jax.random.uniform(jax.random.fold_in(jax.random.fold_in(own_key, 6), dim), (blocks,), jnp.float32, smallest / len(shards), high / len(shards))
        gain = gain * jnp.repeat(jnp.exp(heights), extent[dim] // blocks).reshape((-1,) + (1,) * (len(extent) - 1 - dim))
    return gain


def routed_block(stream_key, own, number, rows, amount, top, most, lean):
    order = jax.random.permutation(stream_key, amount)
    packed, common = load_shares(amount, rows * top, most, lean, True), load_shares(amount, rows * top, most, lean, False)
    places = jnp.arange(amount)

    def named(sizes, turn):
        used = int((sizes > 0).sum())
        fixed = max(1, used // 4)
        shifted = fixed + (places - fixed + turn * (used - fixed)) % max(1, amount - fixed)
        return jnp.zeros((amount,), jnp.int32).at[order[jnp.where(places < fixed, places, shifted)]].set(jnp.asarray(sizes, jnp.int32))

    sizes = jnp.where(number % 4 == 0, named(packed, number // 4), named(common, number - number // 4 - 1))
    mixed = jax.random.permutation(jax.random.fold_in(own, 3), amount)
    giver, receiver = mixed[0:amount // 2 * 2:2], mixed[1:amount // 2 * 2:2]
    slack = jnp.minimum(sizes[giver] - 1, most - sizes[receiver]) // 2
    slack = jnp.where((giver == order[0]) | (receiver == order[0]) | (sizes[receiver] == 0), 0, jnp.maximum(slack, 0))
    shifted = jax.random.randint(jax.random.fold_in(own, 4), (amount // 2,), 0, 1 << 20) % (slack + 1)
    sizes = sizes.at[giver].add(-shifted).at[receiver].add(shifted)
    items = jnp.searchsorted(jnp.cumsum(sizes), jnp.arange(rows * top), side="right").astype(jnp.int32)
    grid = items.reshape(top, rows).T
    grid = grid[jax.random.permutation(jax.random.fold_in(own, 1), rows)]
    turn = jax.random.randint(jax.random.fold_in(own, 2), (rows, 1), 0, top)
    return jnp.take_along_axis(grid, (jnp.arange(top)[None, :] + turn) % top, axis=1)


def load_shares(count, total, reach, slope, full):
    portions = [(1 << 20) // math.isqrt(grade ** slope) + 1 for grade in range(1, count + 1)]
    largest = reach if full else min(reach, max(-(-total // count), total * portions[0] // sum(portions)))
    least = 1 if total - largest >= count - 1 else 0
    given, spare = [largest] + [least] * (count - 1), total - largest - least * (count - 1)
    while spare > 0:
        movable = [i for i in range(1, count) if given[i] < largest] or [i for i in range(1, count) if given[i] < reach]
        mass, budget = sum([portions[i] for i in movable]), spare
        for i in movable:
            addition = min(reach - given[i], max(1, budget * portions[i] // mass), spare)
            given[i] = given[i] + addition
            spare = spare - addition
    return np.array(given)


def normal_values(rng, shape, deviation, reach, split=(), kind=jnp.bfloat16):
    values = deviation * jax.random.normal(rng, shape, jnp.float32)
    if split:
        values = values * level_of(rng, shape, split, -0.22, 0.18)
    return jnp.clip(values, -reach, reach).astype(kind)


def setup_inputs(seed: int = 0) -> dict:
    key_of = jax.random.split(jax.random.key(seed), 9)
    state = normal_values(key_of[0], (FIELDS, NX, NY, NZ), 1.0, 6.0, ((1, 8), (2, 8), (3, 8)))
    diffusivity = jnp.clip(0.25 + 0.75 * jax.random.uniform(key_of[1], (NX, NY, NZ), jnp.float32) ** level_of(key_of[1], (NX, NY, NZ), ((0, 8), (1, 8), (2, 8)), -0.2, 0.2), 0.25, 1.0).astype(jnp.bfloat16)
    coupling = normal_values(key_of[2], (FIELDS, FIELDS), 0.6, 3.0, (), jnp.float32)
    owner_keys = jax.random.split(jax.random.fold_in(key_of[3], 1), BLOCKS // BLK_DEV)
    owner_turns = jax.random.permutation(jax.random.fold_in(key_of[3], 3), BLOCKS // BLK_DEV)
    owner = jax.vmap(lambda own, number: routed_block(jax.random.fold_in(key_of[3], 2), own, number, BLK_DEV, PLANE, 1, SLOT_CAP, 2))(owner_keys, owner_turns).reshape((BLOCKS, 1))
    levels = place_ends(jax.random.randint(key_of[4], (BLOCKS,), 0, 4), jax.random.fold_in(key_of[4], 1), 0, 3).astype(jnp.int32)
    mark_count = jax.random.randint(key_of[5], (1,), BLOCKS // 2, BLOCKS).astype(jnp.int32)
    goal_weight = normal_values(key_of[6], (SLOTS, FIELDS, BX, BY, BZ), 1.0, 6.0, ((0, 512),))
    reaction = jnp.clip(jnp.exp(math.log(2.0) - 1.3862944 * jax.random.uniform(key_of[7], (SLOTS, FIELDS), jnp.float32) ** level_of(key_of[7], (SLOTS, FIELDS), ((0, 512),), -0.2, 0.2)), 0.5, 2.0).astype(jnp.bfloat16)
    return dict(state=state, diffusivity=diffusivity, coupling=coupling, owner=owner, levels=levels, mark_count=mark_count, goal_weight=goal_weight, reaction=reaction)


primal_step = 0.05
dual_step = 0.05


def neighbours(padded):
    center = padded[..., 1:-1, 1:-1, 1:-1]
    summed = padded[..., 2:, 1:-1, 1:-1] + padded[..., :-2, 1:-1, 1:-1]
    summed = summed + padded[..., 1:-1, 2:, 1:-1] + padded[..., 1:-1, :-2, 1:-1]
    summed = summed + padded[..., 1:-1, 1:-1, 2:] + padded[..., 1:-1, 1:-1, :-2]
    return summed - 6.0 * center


def laplace(field):
    widths = [(0, 0)] * (field.ndim - 3) + [(1, 1)] * 3
    return neighbours(jnp.pad(field, widths))


def couple(matrix, field, dim):
    leading = (slice(None),) * dim
    pieces = [field[leading + (col_index,)] for col_index in range(field.shape[dim])]
    combined = []
    for row_index in range(len(pieces)):
        summed = matrix[row_index, 0] * pieces[0]
        for col_index in range(1, len(pieces)):
            summed = summed + matrix[row_index, col_index] * pieces[col_index]
        combined.append(summed)
    return jnp.stack(combined, axis=dim)


def adjoint_sections(diffuse_eff, goal_field, react_rate, coupling):
    transposed = coupling.T
    dual_field = goal_field
    for section_index in range(SECTIONS):
        dual_field = dual_field + dual_step * (diffuse_eff[:, None] * laplace(dual_field) + couple(transposed, dual_field, 1) - react_rate[:, :, None, None, None] * dual_field + goal_field)
    return (dual_field + 0.125 * laplace(dual_field)).astype(jnp.bfloat16)


def to_blocks(field):
    depth = field.shape[0]
    shaped = field.reshape(depth, N_GX, NBX, BX, N_GY, NBY, BY, N_GZ, NBZ, BZ)
    return shaped.transpose(1, 4, 7, 2, 5, 8, 0, 3, 6, 9).reshape(BLOCKS, depth, BX, BY, BZ)


def from_blocks(blocks):
    depth = blocks.shape[1]
    shaped = blocks.reshape(N_GX, N_GY, N_GZ, NBX, NBY, NBZ, depth, BX, BY, BZ)
    return shaped.transpose(6, 0, 3, 7, 1, 4, 8, 2, 5, 9).reshape(depth, NX, NY, NZ)


def reference(state, diffusivity, coupling, owner, levels, mark_count, goal_weight, reaction):
    state_now = state.astype(jnp.float32)
    diffuse = diffusivity.astype(jnp.float32)
    section_one = state_now + primal_step * (diffuse * laplace(state_now) + couple(coupling, state_now, 0))
    residual = diffuse * laplace(section_one) + couple(coupling, section_one, 0) - (section_one - state_now) / primal_step
    effective = (diffuse * (1.0 + 0.5 * jnp.tanh(section_one[0]))).astype(jnp.bfloat16)
    eff_blocks = to_blocks(effective[None])[:, 0]
    res_blocks = to_blocks(residual)
    plane = N_GY * N_GZ
    targets = owner[:, 0].reshape(DEVICES, BLK_DEV)
    order = jnp.arange(BLK_DEV, dtype=jnp.int32)
    same = targets[:, :, None] == targets[:, None, :]
    before = order[None, :] < order[:, None]
    rank = jnp.sum((same & before[None]).astype(jnp.int32), axis=2)
    device_ids = jnp.arange(DEVICES, dtype=jnp.int32)[:, None]
    rows = ((device_ids // plane) * plane + targets) * (plane * SLOT_CAP) + (device_ids % plane) * SLOT_CAP + rank
    rows = rows.reshape(BLOCKS).astype(jnp.int32)
    goal_rows = goal_weight[rows]
    react_rows = reaction[rows]

    def per_device(operands):
        eff_part, goal_part, react_part = operands
        return adjoint_sections(eff_part.astype(jnp.float32), goal_part.astype(jnp.float32), react_part.astype(jnp.float32), coupling)

    enriched = lax.map(per_device, (eff_blocks.reshape(DEVICES, BLK_DEV, BX, BY, BZ), goal_rows.reshape(DEVICES, BLK_DEV, FIELDS, BX, BY, BZ), react_rows.reshape(DEVICES, BLK_DEV, FIELDS)))
    enriched = enriched.reshape(BLOCKS, FIELDS, BX, BY, BZ)
    weights = jnp.exp2(2.0 * levels.astype(jnp.float32))
    indicator = weights * jnp.sum(jnp.abs(res_blocks * enriched.astype(jnp.float32)), axis=(1, 2, 3, 4))
    overall = jnp.sum(indicator)
    share = indicator * BLOCKS / overall
    marked = jnp.minimum(1.0, mark_count[0].astype(jnp.float32) * indicator / overall)
    return from_blocks(enriched), share, marked
```

```python
import jax
import jax.numpy as jnp
from jax import lax
from jax.sharding import PartitionSpec as P

BX = 2
BY = 2
BZ = 128
NBX = 2
NBY = 4
NBZ = 6
SECTIONS = 3
FIELDS = 5


primal_step = 0.05
dual_step = 0.05

REDUCE = "tree"


def faces(cells, sides):
    out = []
    for axis, dim in sides:
        count = lax.axis_size(axis)
        ends = count - 1
        head = lax.slice_in_dim(cells, 0, 1, axis=dim)
        tail = lax.slice_in_dim(cells, cells.shape[dim] - 1, cells.shape[dim], axis=dim)
        below = lax.ppermute(tail, axis, [(i, i + 1) for i in range(ends)])
        above = lax.ppermute(head, axis, [(i + 1, i) for i in range(ends)])
        out.append((below, above))
    return out


def shifted(v, dim, below, above):
    n = v.shape[dim]
    minus = jnp.concatenate([below, lax.slice_in_dim(v, 0, n - 1, axis=dim)], axis=dim)
    plus = jnp.concatenate([lax.slice_in_dim(v, 1, n, axis=dim), above], axis=dim)
    return minus, plus


def laplace_halo(v, halos, dims):
    total = None
    for (below, above), dim in zip(halos, dims):
        minus, plus = shifted(v, dim, below.astype(v.dtype), above.astype(v.dtype))
        pair = minus + plus
        total = pair if total is None else total + pair
    return total - 6.0 * v


def swap_pairs(v, dim):
    shape = v.shape
    split = shape[:dim] + (shape[dim] // 2, 2) + shape[dim + 1:]
    return jnp.flip(v.reshape(split), axis=dim + 1).reshape(shape)


def block_shift(v, dim, width):
    n = v.shape[dim]
    zero = jnp.zeros_like(lax.slice_in_dim(v, 0, 1, axis=dim))
    minus = jnp.concatenate([zero, lax.slice_in_dim(v, 0, n - 1, axis=dim)], axis=dim)
    plus = jnp.concatenate([lax.slice_in_dim(v, 1, n, axis=dim), zero], axis=dim)
    pos = lax.broadcasted_iota(jnp.int32, v.shape, dim) % width
    minus = jnp.where(pos == 0, 0.0, minus)
    plus = jnp.where(pos == width - 1, 0.0, plus)
    return minus + plus


def laplace_blocks(v):
    return swap_pairs(v, 1) + swap_pairs(v, 2) + block_shift(v, 3, BZ) - 6.0 * v


def couple(matrix, v):
    return jnp.sum(matrix[:, :, None, None, None] * v[None], axis=1)


def global_sum(x):
    if REDUCE == "psum":
        return lax.psum(x, ("gx", "gy", "gz"))
    if REDUCE == "gather":
        every = lax.all_gather(x.reshape(1), ("gx", "gy", "gz"), tiled=True)
        return jnp.sum(every)
    for axis in ("gz", "gy", "gx"):
        n = lax.axis_size(axis)
        step = 1
        while step < n:
            x = x + lax.ppermute(x, axis, [(i, (i + step) % n) for i in range(n)])
            step *= 2
    return x


def to_cells(blocks):
    depth = blocks.shape[1]
    shaped = blocks.reshape(NBX, NBY, NBZ, depth, BX, BY, BZ)
    return shaped.transpose(3, 0, 4, 1, 5, 2, 6).reshape(depth, NBX * BX, NBY * BY, NBZ * BZ)


def per_block_cells(values):
    depth = values.shape[1]
    shaped = values.reshape(NBX, NBY, NBZ, depth).transpose(3, 0, 1, 2)
    shaped = jnp.broadcast_to(
        shaped[:, :, None, :, None, :, None], (depth, NBX, BX, NBY, BY, NBZ, BZ)
    )
    return shaped.reshape(depth, NBX * BX, NBY * BY, NBZ * BZ)


def block_sums(cells):
    depth = cells.shape[0]
    shaped = cells.reshape(depth, NBX, BX, NBY, BY, NBZ, BZ)
    return jnp.sum(shaped, axis=(0, 2, 4, 6)).reshape(NBX * NBY * NBZ)


def shards(state, diffusivity, coupling, owner, levels, mark_count, goal_weight, reaction):
    sides = (("gx", 1), ("gy", 2), ("gz", 3))
    dims = (1, 2, 3)

    arrived_goal = lax.all_to_all(goal_weight, ("gy", "gz"), 0, 0, tiled=True)
    arrived_react = lax.all_to_all(reaction, ("gy", "gz"), 0, 0, tiled=True)

    state_now = state.astype(jnp.float32)
    diffuse = diffusivity.astype(jnp.float32)[None]
    state_halo = faces(state, sides)
    section_one = state_now + primal_step * (
        diffuse * laplace_halo(state_now, state_halo, dims) + couple(coupling, state_now)
    )
    section_halo = faces(section_one.astype(jnp.bfloat16), sides)
    residual = (
        diffuse * laplace_halo(section_one, section_halo, dims)
        + couple(coupling, section_one)
        - (section_one - state_now) / primal_step
    )
    effective = (diffuse[0] * (1.0 + 0.5 * jnp.tanh(section_one[0]))).astype(jnp.bfloat16)

    targets = owner[:, 0]
    order = jnp.arange(targets.shape[0], dtype=jnp.int32)
    same = targets[:, None] == targets[None, :]
    before = order[None, :] < order[:, None]
    rank = jnp.sum((same & before).astype(jnp.int32), axis=1)
    capacity = goal_weight.shape[0] // (lax.axis_size("gy") * lax.axis_size("gz"))
    slot_of = targets * capacity + rank

    goal = to_cells(arrived_goal[slot_of]).astype(jnp.float32)
    react = per_block_cells(arrived_react[slot_of]).astype(jnp.float32)
    eff = effective.astype(jnp.float32)[None]
    transposed = coupling.T
    dual = goal
    for _ in range(SECTIONS):
        dual = dual + dual_step * (
            eff * laplace_blocks(dual) + couple(transposed, dual) - react * dual + goal
        )
    enriched = (dual + 0.125 * laplace_blocks(dual)).astype(jnp.bfloat16)

    weights = jnp.exp2(2.0 * levels.astype(jnp.float32))
    indicator = weights * block_sums(jnp.abs(residual * enriched.astype(jnp.float32)))
    overall = global_sum(jnp.sum(indicator))
    block_count = owner.shape[0] * lax.axis_size("gx") * lax.axis_size("gy") * lax.axis_size("gz")
    share = indicator * block_count / overall
    marked = jnp.minimum(1.0, mark_count[0].astype(jnp.float32) * indicator / overall)
    return (enriched, share, marked)


def solution(mesh):
    placed = (
        P(None, "gx", "gy", "gz"),
        P("gx", "gy", "gz"),
        P(),
        P(("gx", "gy", "gz"), None),
        P(("gx", "gy", "gz")),
        P(),
        P(("gx", "gy", "gz"), None, None, None, None),
        P(("gx", "gy", "gz"), None),
    )
    return jax.shard_map(
        shards,
        mesh=mesh,
        in_specs=placed,
        out_specs=(P(None, "gx", "gy", "gz"), P(("gx", "gy", "gz")), P(("gx", "gy", "gz"))),
        check_vma=False,
    )
```

```python
import jax
import jax.numpy as jnp
from jax import lax
from jax.sharding import PartitionSpec as P

BX = 2
BY = 2
BZ = 128
NBX = 2
NBY = 4
NBZ = 6
SECTIONS = 3
FIELDS = 5


primal_step = 0.05
dual_step = 0.05

REDUCE = "exchange"


def faces(cells, sides):
    out = []
    for axis, dim in sides:
        count = lax.axis_size(axis)
        ends = count - 1
        head = lax.slice_in_dim(cells, 0, 1, axis=dim)
        tail = lax.slice_in_dim(cells, cells.shape[dim] - 1, cells.shape[dim], axis=dim)
        below = lax.ppermute(tail, axis, [(i, i + 1) for i in range(ends)])
        above = lax.ppermute(head, axis, [(i + 1, i) for i in range(ends)])
        out.append((below, above))
    return out


def shifted(v, dim, below, above):
    n = v.shape[dim]
    minus = jnp.concatenate([below, lax.slice_in_dim(v, 0, n - 1, axis=dim)], axis=dim)
    plus = jnp.concatenate([lax.slice_in_dim(v, 1, n, axis=dim), above], axis=dim)
    return minus, plus


def laplace_halo(v, halos, dims):
    total = None
    for (below, above), dim in zip(halos, dims):
        minus, plus = shifted(v, dim, below.astype(v.dtype), above.astype(v.dtype))
        pair = minus + plus
        total = pair if total is None else total + pair
    return total - 6.0 * v


def block_shift(v, dim, width):
    n = v.shape[dim]
    zero = jnp.zeros_like(lax.slice_in_dim(v, 0, 1, axis=dim))
    minus = jnp.concatenate([zero, lax.slice_in_dim(v, 0, n - 1, axis=dim)], axis=dim)
    plus = jnp.concatenate([lax.slice_in_dim(v, 1, n, axis=dim), zero], axis=dim)
    pos = lax.broadcasted_iota(jnp.int32, v.shape, dim) % width
    minus = jnp.where(pos == 0, 0.0, minus)
    plus = jnp.where(pos == width - 1, 0.0, plus)
    return minus + plus


def laplace_blocks(v):
    return block_shift(v, 1, BX) + block_shift(v, 2, BY) + block_shift(v, 3, BZ) - 6.0 * v


def couple(matrix, v):
    return jnp.sum(matrix[:, :, None, None, None] * v[None], axis=1)


def global_sum(x):
    if REDUCE == "psum":
        return lax.psum(x, ("gx", "gy", "gz"))
    if REDUCE == "exchange":
        for group in (("gy", "gz"), ("gx",)):
            count = 1
            for axis in group:
                count *= lax.axis_size(axis)
            spread = jnp.broadcast_to(x.reshape(1), (count,))
            x = jnp.sum(lax.all_to_all(spread, group, 0, 0, tiled=True))
        return x
    if REDUCE == "gather":
        every = lax.all_gather(x.reshape(1), ("gx", "gy", "gz"), tiled=True)
        return jnp.sum(every)
    for axis in ("gz", "gy", "gx"):
        n = lax.axis_size(axis)
        step = 1
        while step < n:
            x = x + lax.ppermute(x, axis, [(i, (i + step) % n) for i in range(n)])
            step *= 2
    return x


def to_cells(blocks):
    depth = blocks.shape[1]
    shaped = blocks.reshape(NBX, NBY, NBZ, depth, BX, BY, BZ)
    return shaped.transpose(3, 0, 4, 1, 5, 2, 6).reshape(depth, NBX * BX, NBY * BY, NBZ * BZ)


def per_block_cells(values):
    depth = values.shape[1]
    shaped = values.reshape(NBX, NBY, NBZ, depth).transpose(3, 0, 1, 2)
    shaped = jnp.broadcast_to(
        shaped[:, :, None, :, None, :, None], (depth, NBX, BX, NBY, BY, NBZ, BZ)
    )
    return shaped.reshape(depth, NBX * BX, NBY * BY, NBZ * BZ)


def block_sums(cells):
    depth = cells.shape[0]
    shaped = cells.reshape(depth, NBX, BX, NBY, BY, NBZ, BZ)
    return jnp.sum(shaped, axis=(0, 2, 4, 6)).reshape(NBX * NBY * NBZ)


def shards(state, diffusivity, coupling, owner, levels, mark_count, goal_weight, reaction):
    sides = (("gx", 1), ("gy", 2), ("gz", 3))
    dims = (1, 2, 3)

    slots = goal_weight.shape[0]
    packed = jnp.concatenate(
        [
            goal_weight.reshape(slots, FIELDS, BX * BY, BZ),
            jnp.broadcast_to(reaction[:, :, None, None], (slots, FIELDS, 1, BZ)),
        ],
        axis=2,
    )
    arrived = lax.all_to_all(packed, ("gy", "gz"), 0, 0, tiled=True)

    state_now = state.astype(jnp.float32)
    diffuse = diffusivity.astype(jnp.float32)[None]
    state_halo = faces(state, sides)
    section_one = state_now + primal_step * (
        diffuse * laplace_halo(state_now, state_halo, dims) + couple(coupling, state_now)
    )
    section_halo = faces(section_one.astype(jnp.bfloat16), sides)
    residual = (
        diffuse * laplace_halo(section_one, section_halo, dims)
        + couple(coupling, section_one)
        - (section_one - state_now) / primal_step
    )
    effective = (diffuse[0] * (1.0 + 0.5 * jnp.tanh(section_one[0]))).astype(jnp.bfloat16)

    targets = owner[:, 0]
    order = jnp.arange(targets.shape[0], dtype=jnp.int32)
    same = targets[:, None] == targets[None, :]
    before = order[None, :] < order[:, None]
    rank = jnp.sum((same & before).astype(jnp.int32), axis=1)
    capacity = goal_weight.shape[0] // (lax.axis_size("gy") * lax.axis_size("gz"))
    slot_of = targets * capacity + rank

    mine = arrived[slot_of]
    goal = to_cells(mine[:, :, : BX * BY].reshape(-1, FIELDS, BX, BY, BZ)).astype(jnp.float32)
    react = per_block_cells(mine[:, :, BX * BY, 0]).astype(jnp.float32)
    eff = effective.astype(jnp.float32)[None]
    transposed = coupling.T
    dual = goal
    for _ in range(SECTIONS):
        dual = dual + dual_step * (
            eff * laplace_blocks(dual) + couple(transposed, dual) - react * dual + goal
        )
    enriched = (dual + 0.125 * laplace_blocks(dual)).astype(jnp.bfloat16)

    weights = jnp.exp2(2.0 * levels.astype(jnp.float32))
    indicator = weights * block_sums(jnp.abs(residual * enriched.astype(jnp.float32)))
    overall = global_sum(jnp.sum(indicator))
    block_count = owner.shape[0] * lax.axis_size("gx") * lax.axis_size("gy") * lax.axis_size("gz")
    share = indicator * block_count / overall
    marked = jnp.minimum(1.0, mark_count[0].astype(jnp.float32) * indicator / overall)
    return (enriched, share, marked)


def solution(mesh):
    placed = (
        P(None, "gx", "gy", "gz"),
        P("gx", "gy", "gz"),
        P(),
        P(("gx", "gy", "gz"), None),
        P(("gx", "gy", "gz")),
        P(),
        P(("gx", "gy", "gz"), None, None, None, None),
        P(("gx", "gy", "gz"), None),
    )
    return jax.shard_map(
        shards,
        mesh=mesh,
        in_specs=placed,
        out_specs=(P(None, "gx", "gy", "gz"), P(("gx", "gy", "gz")), P(("gx", "gy", "gz"))),
        check_vma=False,
    )
```

```python
import jax
import jax.numpy as jnp
from jax import lax
from jax.experimental import pallas as pl
from jax.experimental.pallas import tpu as pltpu
from jax.sharding import PartitionSpec as P

BX = 2
BY = 2
BZ = 128
NBX = 2
NBY = 4
NBZ = 6
SECTIONS = 3
FIELDS = 5


primal_step = 0.05
dual_step = 0.05

REDUCE = "exchange"


def faces(cells, sides):
    out = []
    for axis, dim in sides:
        count = lax.axis_size(axis)
        ends = count - 1
        head = lax.slice_in_dim(cells, 0, 1, axis=dim)
        tail = lax.slice_in_dim(cells, cells.shape[dim] - 1, cells.shape[dim], axis=dim)
        below = lax.ppermute(tail, axis, [(i, i + 1) for i in range(ends)])
        above = lax.ppermute(head, axis, [(i + 1, i) for i in range(ends)])
        out.append((below, above))
    return out


def shifted(v, dim, below, above):
    n = v.shape[dim]
    minus = jnp.concatenate([below, lax.slice_in_dim(v, 0, n - 1, axis=dim)], axis=dim)
    plus = jnp.concatenate([lax.slice_in_dim(v, 1, n, axis=dim), above], axis=dim)
    return minus, plus


def laplace_halo(v, halos, dims):
    total = None
    for (below, above), dim in zip(halos, dims):
        minus, plus = shifted(v, dim, below.astype(v.dtype), above.astype(v.dtype))
        pair = minus + plus
        total = pair if total is None else total + pair
    return total - 6.0 * v


def block_shift(v, dim, width):
    n = v.shape[dim]
    zero = jnp.zeros_like(lax.slice_in_dim(v, 0, 1, axis=dim))
    minus = jnp.concatenate([zero, lax.slice_in_dim(v, 0, n - 1, axis=dim)], axis=dim)
    plus = jnp.concatenate([lax.slice_in_dim(v, 1, n, axis=dim), zero], axis=dim)
    pos = lax.broadcasted_iota(jnp.int32, v.shape, dim) % width
    minus = jnp.where(pos == 0, 0.0, minus)
    plus = jnp.where(pos == width - 1, 0.0, plus)
    return minus + plus


def laplace_blocks(v):
    return block_shift(v, 1, BX) + block_shift(v, 2, BY) + block_shift(v, 3, BZ) - 6.0 * v


def couple(matrix, v):
    return jnp.sum(matrix[:, :, None, None, None] * v[None], axis=1)


def global_sum(x):
    if REDUCE == "psum":
        return lax.psum(x, ("gx", "gy", "gz"))
    if REDUCE == "exchange":
        for group in (("gy", "gz"), ("gx",)):
            count = 1
            for axis in group:
                count *= lax.axis_size(axis)
            spread = jnp.broadcast_to(x.reshape(1), (count,))
            x = jnp.sum(lax.all_to_all(spread, group, 0, 0, tiled=True))
        return x
    if REDUCE == "gather":
        every = lax.all_gather(x.reshape(1), ("gx", "gy", "gz"), tiled=True)
        return jnp.sum(every)
    for axis in ("gz", "gy", "gx"):
        n = lax.axis_size(axis)
        step = 1
        while step < n:
            x = x + lax.ppermute(x, axis, [(i, (i + step) % n) for i in range(n)])
            step *= 2
    return x


def to_cells(blocks):
    depth = blocks.shape[1]
    shaped = blocks.reshape(NBX, NBY, NBZ, depth, BX, BY, BZ)
    return shaped.transpose(3, 0, 4, 1, 5, 2, 6).reshape(depth, NBX * BX, NBY * BY, NBZ * BZ)


def per_block_cells(values):
    depth = values.shape[1]
    shaped = values.reshape(NBX, NBY, NBZ, depth).transpose(3, 0, 1, 2)
    shaped = jnp.broadcast_to(
        shaped[:, :, None, :, None, :, None], (depth, NBX, BX, NBY, BY, NBZ, BZ)
    )
    return shaped.reshape(depth, NBX * BX, NBY * BY, NBZ * BZ)


def block_sums(cells):
    depth = cells.shape[0]
    shaped = cells.reshape(depth, NBX, BX, NBY, BY, NBZ, BZ)
    return jnp.sum(shaped, axis=(0, 2, 4, 6)).reshape(NBX * NBY * NBZ)


def _masks(rows_n, lanes_n):
    rows = lax.broadcasted_iota(jnp.int32, (rows_n, lanes_n), 0)
    lanes = lax.broadcasted_iota(jnp.int32, (rows_n, lanes_n), 1)
    r_src = (pltpu.roll(rows, 1, 0), pltpu.roll(rows, rows_n - 1, 0))
    l_src = (pltpu.roll(lanes, 1, 1), pltpu.roll(lanes, lanes_n - 1, 1))
    return rows, lanes, r_src, l_src


def _rolled(v):
    rows_n, lanes_n = v.shape
    return (
        (pltpu.roll(v, 1, 0), pltpu.roll(v, rows_n - 1, 0)),
        (pltpu.roll(v, 1, 1), pltpu.roll(v, lanes_n - 1, 1)),
    )


def _lap_halo(c, xm, xp, ylo, yhi, zlo, zhi, geo):
    rows, lanes, r_src, l_src = geo
    rows_n, lanes_n = c.shape
    (r1, r2), (l1, l2) = _rolled(c)
    y_out = jnp.where(rows == 0, ylo, yhi)
    z_out = jnp.where(lanes == 0, zlo, zhi)
    t1 = jnp.where(jnp.abs(r_src[0] - rows) == 1, r1, y_out)
    t2 = jnp.where(jnp.abs(r_src[1] - rows) == 1, r2, y_out)
    u1 = jnp.where(jnp.abs(l_src[0] - lanes) == 1, l1, z_out)
    u2 = jnp.where(jnp.abs(l_src[1] - lanes) == 1, l2, z_out)
    return (xp + xm) + (t1 + t2) + (u1 + u2) - 6.0 * c


def _lap_block(c, partner_x, geo):
    rows, lanes, r_src, l_src = geo
    (r1, r2), (l1, l2) = _rolled(c)
    t1 = jnp.where(r_src[0] // BY == rows // BY, r1, 0.0)
    t2 = jnp.where(r_src[1] // BY == rows // BY, r2, 0.0)
    u1 = jnp.where(l_src[0] // BZ == lanes // BZ, l1, 0.0)
    u2 = jnp.where(l_src[1] // BZ == lanes // BZ, l2, 0.0)
    return partner_x + (t1 + t2) + (u1 + u2) - 6.0 * c


def _couple(c_ref, vals, transpose):
    out = []
    for f in range(len(vals)):
        def m(g):
            return c_ref[g, f] if transpose else c_ref[f, g]
        acc = m(0) * vals[0]
        for g in range(1, len(vals)):
            acc = acc + m(g) * vals[g]
        out.append(acc)
    return out


def primal_kernel(c_ref, s_ref, d_ref, xlo, xhi, ylo, yhi, zlo, zhi,
                  s1_ref, eff_ref, oxlo, oxhi, oylo, oyhi, ozlo, ozhi):
    nf, nx, ny, nz = s_ref.shape
    geo = _masks(ny, nz)
    f32 = jnp.float32
    s = [[s_ref[f, x].astype(f32) for x in range(nx)] for f in range(nf)]
    for x in range(nx):
        d = d_ref[x].astype(f32)
        col = [s[f][x] for f in range(nf)]
        cs = _couple(c_ref, col, False)
        s1 = []
        for f in range(nf):
            xm = s[f][x - 1] if x > 0 else xlo[f, 0].astype(f32)
            xp = s[f][x + 1] if x < nx - 1 else xhi[f, 0].astype(f32)
            lap = _lap_halo(s[f][x], xm, xp, ylo[f, x].astype(f32), yhi[f, x].astype(f32),
                            zlo[f, x].astype(f32), zhi[f, x].astype(f32), geo)
            v = s[f][x] + primal_step * (d * lap + cs[f])
            s1.append(v)
            s1_ref[f, x] = v
            low = v.astype(jnp.bfloat16)
            if x == 0:
                oxlo[f, 0] = low
            if x == nx - 1:
                oxhi[f, 0] = low
            oylo[f, x] = low[0:1, :]
            oyhi[f, x] = low[ny - 1:ny, :]
            ozlo[f, x] = low[:, 0:1]
            ozhi[f, x] = low[:, nz - 1:nz]
        eff_ref[x] = (d * (1.0 + 0.5 * jnp.tanh(s1[0]))).astype(jnp.bfloat16)


def adjoint_kernel(c_ref, s1_ref, s_ref, d_ref, xlo, xhi, ylo, yhi, zlo, zhi, eff_ref, goal_ref, react_ref,
                   enr_ref, part_ref):
    nf, nx, ny, nz = s_ref.shape
    geo = _masks(ny, nz)
    f32 = jnp.float32
    s1 = [[s1_ref[f, x] for x in range(nx)] for f in range(nf)]
    residual = [[None] * nx for _ in range(nf)]
    for x in range(nx):
        d = d_ref[x].astype(f32)
        cs = _couple(c_ref, [s1[f][x] for f in range(nf)], False)
        for f in range(nf):
            xm = s1[f][x - 1] if x > 0 else xlo[f, 0].astype(f32)
            xp = s1[f][x + 1] if x < nx - 1 else xhi[f, 0].astype(f32)
            lap = _lap_halo(s1[f][x], xm, xp, ylo[f, x].astype(f32), yhi[f, x].astype(f32),
                            zlo[f, x].astype(f32), zhi[f, x].astype(f32), geo)
            residual[f][x] = d * lap + cs[f] - (s1[f][x] - s_ref[f, x].astype(f32)) / primal_step
    eff = [eff_ref[x].astype(f32) for x in range(nx)]
    goal = [[goal_ref[f, x].astype(f32) for x in range(nx)] for f in range(nf)]
    react = [[react_ref[f, x].astype(f32) for x in range(nx)] for f in range(nf)]
    dual = [list(row) for row in goal]
    for _ in range(SECTIONS):
        new = [[None] * nx for _ in range(nf)]
        for x in range(nx):
            ct = _couple(c_ref, [dual[f][x] for f in range(nf)], True)
            for f in range(nf):
                lap = _lap_block(dual[f][x], dual[f][x ^ 1], geo)
                new[f][x] = dual[f][x] + dual_step * (
                    eff[x] * lap + ct[f] - react[f][x] * dual[f][x] + goal[f][x]
                )
        dual = new
    for bx in range(nx // BX):
        acc = None
        for x in range(bx * BX, bx * BX + BX):
            for f in range(nf):
                lap = _lap_block(dual[f][x], dual[f][x ^ 1], geo)
                e = (dual[f][x] + 0.125 * lap).astype(jnp.bfloat16)
                enr_ref[f, x] = e
                term = jnp.abs(residual[f][x] * e.astype(f32))
                acc = term if acc is None else acc + term
        part_ref[bx] = acc


def shards(state, diffusivity, coupling, owner, levels, mark_count, goal_weight, reaction):
    sides = (("gx", 1), ("gy", 2), ("gz", 3))
    dims = (1, 2, 3)

    slots = goal_weight.shape[0]
    packed = jnp.concatenate(
        [
            goal_weight.reshape(slots, FIELDS, BX * BY, BZ),
            jnp.broadcast_to(reaction[:, :, None, None], (slots, FIELDS, 1, BZ)),
        ],
        axis=2,
    )
    arrived = lax.all_to_all(packed, ("gy", "gz"), 0, 0, tiled=True)

    f32, bf16 = jnp.float32, jnp.bfloat16
    nf, nx, ny, nz = state.shape
    vmem = pl.BlockSpec(memory_space=pltpu.VMEM)
    smem = pl.BlockSpec(memory_space=pltpu.SMEM)
    face_shapes = [(nf, 1, ny, nz)] * 2 + [(nf, nx, 1, nz)] * 2 + [(nf, nx, ny, 1)] * 2
    state_halo = [h for pair in faces(state, sides) for h in pair]
    primal = pl.pallas_call(
        primal_kernel,
        out_shape=[jax.ShapeDtypeStruct(state.shape, f32), jax.ShapeDtypeStruct((nx, ny, nz), bf16)]
        + [jax.ShapeDtypeStruct(shape, bf16) for shape in face_shapes],
        in_specs=[smem] + [vmem] * 8,
        out_specs=[vmem] * 8,
    )(coupling, state, diffusivity, *state_halo)
    section_one, effective = primal[0], primal[1]
    section_halo = []
    for (axis, _), low, high in zip(sides, primal[2::2], primal[3::2]):
        ends = lax.axis_size(axis) - 1
        section_halo.append(lax.ppermute(high, axis, [(i, i + 1) for i in range(ends)]))
        section_halo.append(lax.ppermute(low, axis, [(i + 1, i) for i in range(ends)]))

    targets = owner[:, 0]
    order = jnp.arange(targets.shape[0], dtype=jnp.int32)
    same = targets[:, None] == targets[None, :]
    before = order[None, :] < order[:, None]
    rank = jnp.sum((same & before).astype(jnp.int32), axis=1)
    capacity = goal_weight.shape[0] // (lax.axis_size("gy") * lax.axis_size("gz"))
    slot_of = targets * capacity + rank

    mine = arrived[slot_of]
    goal = to_cells(mine[:, :, : BX * BY].reshape(-1, FIELDS, BX, BY, BZ))
    react = per_block_cells(mine[:, :, BX * BY, 0])
    enriched, part = pl.pallas_call(
        adjoint_kernel,
        out_shape=[jax.ShapeDtypeStruct(state.shape, bf16), jax.ShapeDtypeStruct((nx // BX, ny, nz), f32)],
        in_specs=[smem] + [vmem] * 12,
        out_specs=[vmem] * 2,
    )(coupling, section_one, state, diffusivity, *section_halo, effective, goal, react)
    sums = jnp.sum(part.reshape(nx // BX, ny // BY, BY, nz // BZ, BZ), axis=(2, 4)).reshape(-1)

    weights = jnp.exp2(2.0 * levels.astype(jnp.float32))
    indicator = weights * sums
    overall = global_sum(jnp.sum(indicator))
    block_count = owner.shape[0] * lax.axis_size("gx") * lax.axis_size("gy") * lax.axis_size("gz")
    share = indicator * block_count / overall
    marked = jnp.minimum(1.0, mark_count[0].astype(jnp.float32) * indicator / overall)
    return (enriched, share, marked)


def solution(mesh):
    placed = (
        P(None, "gx", "gy", "gz"),
        P("gx", "gy", "gz"),
        P(),
        P(("gx", "gy", "gz"), None),
        P(("gx", "gy", "gz")),
        P(),
        P(("gx", "gy", "gz"), None, None, None, None),
        P(("gx", "gy", "gz"), None),
    )
    return jax.shard_map(
        shards,
        mesh=mesh,
        in_specs=placed,
        out_specs=(P(None, "gx", "gy", "gz"), P(("gx", "gy", "gz")), P(("gx", "gy", "gz"))),
        check_vma=False,
    )
```

```python
import jax
import jax.numpy as jnp
from jax import lax
from jax.experimental import pallas as pl
from jax.experimental.pallas import tpu as pltpu
from jax.sharding import PartitionSpec as P

BX = 2
BY = 2
BZ = 128
NBX = 2
NBY = 4
NBZ = 6
SECTIONS = 3
FIELDS = 5


primal_step = 0.05
dual_step = 0.05

REDUCE = "exchange"


def faces(cells, sides):
    out = []
    for axis, dim in sides:
        count = lax.axis_size(axis)
        ends = count - 1
        head = lax.slice_in_dim(cells, 0, 1, axis=dim)
        tail = lax.slice_in_dim(cells, cells.shape[dim] - 1, cells.shape[dim], axis=dim)
        below = lax.ppermute(tail, axis, [(i, i + 1) for i in range(ends)])
        above = lax.ppermute(head, axis, [(i + 1, i) for i in range(ends)])
        out.append((below, above))
    return out


def shifted(v, dim, below, above):
    n = v.shape[dim]
    minus = jnp.concatenate([below, lax.slice_in_dim(v, 0, n - 1, axis=dim)], axis=dim)
    plus = jnp.concatenate([lax.slice_in_dim(v, 1, n, axis=dim), above], axis=dim)
    return minus, plus


def laplace_halo(v, halos, dims):
    total = None
    for (below, above), dim in zip(halos, dims):
        minus, plus = shifted(v, dim, below.astype(v.dtype), above.astype(v.dtype))
        pair = minus + plus
        total = pair if total is None else total + pair
    return total - 6.0 * v


def block_shift(v, dim, width):
    n = v.shape[dim]
    zero = jnp.zeros_like(lax.slice_in_dim(v, 0, 1, axis=dim))
    minus = jnp.concatenate([zero, lax.slice_in_dim(v, 0, n - 1, axis=dim)], axis=dim)
    plus = jnp.concatenate([lax.slice_in_dim(v, 1, n, axis=dim), zero], axis=dim)
    pos = lax.broadcasted_iota(jnp.int32, v.shape, dim) % width
    minus = jnp.where(pos == 0, 0.0, minus)
    plus = jnp.where(pos == width - 1, 0.0, plus)
    return minus + plus


def laplace_blocks(v):
    return block_shift(v, 1, BX) + block_shift(v, 2, BY) + block_shift(v, 3, BZ) - 6.0 * v


def couple(matrix, v):
    return jnp.sum(matrix[:, :, None, None, None] * v[None], axis=1)


def global_sum(x):
    if REDUCE == "psum":
        return lax.psum(x, ("gx", "gy", "gz"))
    if REDUCE == "exchange":
        for group in (("gy", "gz"), ("gx",)):
            count = 1
            for axis in group:
                count *= lax.axis_size(axis)
            spread = jnp.broadcast_to(x.reshape(1), (count,))
            x = jnp.sum(lax.all_to_all(spread, group, 0, 0, tiled=True))
        return x
    if REDUCE == "gather":
        every = lax.all_gather(x.reshape(1), ("gx", "gy", "gz"), tiled=True)
        return jnp.sum(every)
    for axis in ("gz", "gy", "gx"):
        n = lax.axis_size(axis)
        step = 1
        while step < n:
            x = x + lax.ppermute(x, axis, [(i, (i + step) % n) for i in range(n)])
            step *= 2
    return x


def to_cells(blocks):
    depth = blocks.shape[1]
    shaped = blocks.reshape(NBX, NBY, NBZ, depth, BX, BY, BZ)
    return shaped.transpose(3, 0, 4, 1, 5, 2, 6).reshape(depth, NBX * BX, NBY * BY, NBZ * BZ)


def per_block_cells(values):
    depth = values.shape[1]
    shaped = values.reshape(NBX, NBY, NBZ, depth).transpose(3, 0, 1, 2)
    shaped = jnp.broadcast_to(
        shaped[:, :, None, :, None, :, None], (depth, NBX, BX, NBY, BY, NBZ, BZ)
    )
    return shaped.reshape(depth, NBX * BX, NBY * BY, NBZ * BZ)


def block_sums(cells):
    depth = cells.shape[0]
    shaped = cells.reshape(depth, NBX, BX, NBY, BY, NBZ, BZ)
    return jnp.sum(shaped, axis=(0, 2, 4, 6)).reshape(NBX * NBY * NBZ)


def _masks(rows_n, lanes_n):
    rows = lax.broadcasted_iota(jnp.int32, (rows_n, lanes_n), 0)
    lanes = lax.broadcasted_iota(jnp.int32, (rows_n, lanes_n), 1)
    r_src = (pltpu.roll(rows, 1, 0), pltpu.roll(rows, rows_n - 1, 0))
    l_src = (pltpu.roll(lanes, 1, 1), pltpu.roll(lanes, lanes_n - 1, 1))
    return rows, lanes, r_src, l_src


def _rolled(v):
    rows_n, lanes_n = v.shape
    return (
        (pltpu.roll(v, 1, 0), pltpu.roll(v, rows_n - 1, 0)),
        (pltpu.roll(v, 1, 1), pltpu.roll(v, lanes_n - 1, 1)),
    )


def _lap_halo(c, xm, xp, ylo, yhi, zlo, zhi, geo):
    rows, lanes, r_src, l_src = geo
    rows_n, lanes_n = c.shape
    (r1, r2), (l1, l2) = _rolled(c)
    y_out = jnp.where(rows == 0, ylo, yhi)
    z_out = jnp.where(lanes == 0, zlo, zhi)
    t1 = jnp.where(jnp.abs(r_src[0] - rows) == 1, r1, y_out)
    t2 = jnp.where(jnp.abs(r_src[1] - rows) == 1, r2, y_out)
    u1 = jnp.where(jnp.abs(l_src[0] - lanes) == 1, l1, z_out)
    u2 = jnp.where(jnp.abs(l_src[1] - lanes) == 1, l2, z_out)
    return (xp + xm) + (t1 + t2) + (u1 + u2) - 6.0 * c


def _lap_block(c, partner_x, geo):
    rows, lanes, r_src, l_src = geo
    (r1, r2), (l1, l2) = _rolled(c)
    t1 = jnp.where(r_src[0] // BY == rows // BY, r1, 0.0)
    t2 = jnp.where(r_src[1] // BY == rows // BY, r2, 0.0)
    u1 = jnp.where(l_src[0] // BZ == lanes // BZ, l1, 0.0)
    u2 = jnp.where(l_src[1] // BZ == lanes // BZ, l2, 0.0)
    return partner_x + (t1 + t2) + (u1 + u2) - 6.0 * c


def _couple(c_ref, vals, transpose):
    out = []
    for f in range(len(vals)):
        def m(g):
            return c_ref[g, f] if transpose else c_ref[f, g]
        acc = m(0) * vals[0]
        for g in range(1, len(vals)):
            acc = acc + m(g) * vals[g]
        out.append(acc)
    return out


def primal_kernel(c_ref, s_ref, d_ref, xlo, xhi, ylo, yhi, zlo, zhi,
                  s1_ref, eff_ref, oxlo, oxhi, oylo, oyhi, ozlo, ozhi):
    nf, nx, ny, nz = s_ref.shape
    geo = _masks(ny, nz)
    f32 = jnp.float32
    s = [[s_ref[f, x].astype(f32) for x in range(nx)] for f in range(nf)]
    for x in range(nx):
        d = d_ref[x].astype(f32)
        col = [s[f][x] for f in range(nf)]
        cs = _couple(c_ref, col, False)
        s1 = []
        for f in range(nf):
            xm = s[f][x - 1] if x > 0 else xlo[f, 0].astype(f32)
            xp = s[f][x + 1] if x < nx - 1 else xhi[f, 0].astype(f32)
            lap = _lap_halo(s[f][x], xm, xp, ylo[f, x].astype(f32), yhi[f, x].astype(f32),
                            zlo[f, x].astype(f32), zhi[f, x].astype(f32), geo)
            v = s[f][x] + primal_step * (d * lap + cs[f])
            s1.append(v)
            s1_ref[f, x] = v
            low = v.astype(jnp.bfloat16)
            if x == 0:
                oxlo[f, 0] = low
            if x == nx - 1:
                oxhi[f, 0] = low
            oylo[f, x] = low[0:1, :]
            oyhi[f, x] = low[ny - 1:ny, :]
            ozlo[f, x] = low[:, 0:1]
            ozhi[f, x] = low[:, nz - 1:nz]
        eff_ref[x] = (d * (1.0 + 0.5 * jnp.tanh(s1[0]))).astype(jnp.bfloat16)


def adjoint_kernel(c_ref, s1_ref, s_ref, d_ref, xlo, xhi, ylo, yhi, zlo, zhi, eff_ref, goal_ref, react_ref,
                   enr_ref, part_ref):
    nf, nx, ny, nz = s_ref.shape
    geo = _masks(ny, nz)
    f32 = jnp.float32
    s1 = [[s1_ref[f, x] for x in range(nx)] for f in range(nf)]
    residual = [[None] * nx for _ in range(nf)]
    for x in range(nx):
        d = d_ref[x].astype(f32)
        cs = _couple(c_ref, [s1[f][x] for f in range(nf)], False)
        for f in range(nf):
            xm = s1[f][x - 1] if x > 0 else xlo[f, 0].astype(f32)
            xp = s1[f][x + 1] if x < nx - 1 else xhi[f, 0].astype(f32)
            lap = _lap_halo(s1[f][x], xm, xp, ylo[f, x].astype(f32), yhi[f, x].astype(f32),
                            zlo[f, x].astype(f32), zhi[f, x].astype(f32), geo)
            residual[f][x] = d * lap + cs[f] - (s1[f][x] - s_ref[f, x].astype(f32)) / primal_step
    eff = [eff_ref[x].astype(f32) for x in range(nx)]
    goal = [[goal_ref[f, x].astype(f32) for x in range(nx)] for f in range(nf)]
    react = [[react_ref[f, x].astype(f32) for x in range(nx)] for f in range(nf)]
    dual = [list(row) for row in goal]
    for _ in range(SECTIONS):
        new = [[None] * nx for _ in range(nf)]
        for x in range(nx):
            ct = _couple(c_ref, [dual[f][x] for f in range(nf)], True)
            for f in range(nf):
                lap = _lap_block(dual[f][x], dual[f][x ^ 1], geo)
                new[f][x] = dual[f][x] + dual_step * (
                    eff[x] * lap + ct[f] - react[f][x] * dual[f][x] + goal[f][x]
                )
        dual = new
    for bx in range(nx // BX):
        acc = None
        for x in range(bx * BX, bx * BX + BX):
            for f in range(nf):
                lap = _lap_block(dual[f][x], dual[f][x ^ 1], geo)
                e = (dual[f][x] + 0.125 * lap).astype(jnp.bfloat16)
                enr_ref[f, x] = e
                term = jnp.abs(residual[f][x] * e.astype(f32))
                acc = term if acc is None else acc + term
        part_ref[bx] = acc


def shards(state, diffusivity, coupling, owner, levels, mark_count, goal_weight, reaction):
    sides = (("gx", 1), ("gy", 2), ("gz", 3))
    dims = (1, 2, 3)

    slots = goal_weight.shape[0]
    packed = jnp.concatenate(
        [
            goal_weight.reshape(slots, FIELDS, BX * BY, BZ),
            jnp.broadcast_to(reaction[:, :, None, None], (slots, FIELDS, 1, BZ)),
        ],
        axis=2,
    )

    f32, bf16 = jnp.float32, jnp.bfloat16
    nf, nx, ny, nz = state.shape
    vmem = pl.BlockSpec(memory_space=pltpu.VMEM)
    smem = pl.BlockSpec(memory_space=pltpu.SMEM)
    face_shapes = [(nf, 1, ny, nz)] * 2 + [(nf, nx, 1, nz)] * 2 + [(nf, nx, ny, 1)] * 2
    state_halo = [h for pair in faces(state, sides) for h in pair]
    packed, *state_halo = lax.optimization_barrier((packed, *state_halo))
    arrived = lax.all_to_all(packed, ("gy", "gz"), 0, 0, tiled=True)
    primal = pl.pallas_call(
        primal_kernel,
        out_shape=[jax.ShapeDtypeStruct(state.shape, f32), jax.ShapeDtypeStruct((nx, ny, nz), bf16)]
        + [jax.ShapeDtypeStruct(shape, bf16) for shape in face_shapes],
        in_specs=[smem] + [vmem] * 8,
        out_specs=[vmem] * 8,
    )(coupling, state, diffusivity, *state_halo)
    section_one, effective = primal[0], primal[1]
    section_halo = []
    for (axis, _), low, high in zip(sides, primal[2::2], primal[3::2]):
        ends = lax.axis_size(axis) - 1
        section_halo.append(lax.ppermute(high, axis, [(i, i + 1) for i in range(ends)]))
        section_halo.append(lax.ppermute(low, axis, [(i + 1, i) for i in range(ends)]))

    targets = owner[:, 0]
    order = jnp.arange(targets.shape[0], dtype=jnp.int32)
    same = targets[:, None] == targets[None, :]
    before = order[None, :] < order[:, None]
    rank = jnp.sum((same & before).astype(jnp.int32), axis=1)
    capacity = goal_weight.shape[0] // (lax.axis_size("gy") * lax.axis_size("gz"))
    slot_of = targets * capacity + rank

    mine = arrived[slot_of]
    goal = to_cells(mine[:, :, : BX * BY].reshape(-1, FIELDS, BX, BY, BZ))
    react = per_block_cells(mine[:, :, BX * BY, 0])
    enriched, part = pl.pallas_call(
        adjoint_kernel,
        out_shape=[jax.ShapeDtypeStruct(state.shape, bf16), jax.ShapeDtypeStruct((nx // BX, ny, nz), f32)],
        in_specs=[smem] + [vmem] * 12,
        out_specs=[vmem] * 2,
    )(coupling, section_one, state, diffusivity, *section_halo, effective, goal, react)
    sums = jnp.sum(part.reshape(nx // BX, ny // BY, BY, nz // BZ, BZ), axis=(2, 4)).reshape(-1)

    weights = jnp.exp2(2.0 * levels.astype(jnp.float32))
    indicator = weights * sums
    overall = global_sum(jnp.sum(indicator))
    block_count = owner.shape[0] * lax.axis_size("gx") * lax.axis_size("gy") * lax.axis_size("gz")
    share = indicator * block_count / overall
    marked = jnp.minimum(1.0, mark_count[0].astype(jnp.float32) * indicator / overall)
    return (enriched, share, marked)


def solution(mesh):
    placed = (
        P(None, "gx", "gy", "gz"),
        P("gx", "gy", "gz"),
        P(),
        P(("gx", "gy", "gz"), None),
        P(("gx", "gy", "gz")),
        P(),
        P(("gx", "gy", "gz"), None, None, None, None),
        P(("gx", "gy", "gz"), None),
    )
    return jax.shard_map(
        shards,
        mesh=mesh,
        in_specs=placed,
        out_specs=(P(None, "gx", "gy", "gz"), P(("gx", "gy", "gz")), P(("gx", "gy", "gz"))),
        check_vma=False,
    )
```

```python
import jax
import jax.numpy as jnp
from jax import lax
from jax.experimental import pallas as pl
from jax.experimental.pallas import tpu as pltpu
from jax.sharding import PartitionSpec as P

BX = 2
BY = 2
BZ = 128
NBX = 2
NBY = 4
NBZ = 6
SECTIONS = 3
FIELDS = 5


primal_step = 0.05
dual_step = 0.05

REDUCE = "exchange"


def faces(cells, sides):
    out = []
    for axis, dim in sides:
        count = lax.axis_size(axis)
        ends = count - 1
        head = lax.slice_in_dim(cells, 0, 1, axis=dim)
        tail = lax.slice_in_dim(cells, cells.shape[dim] - 1, cells.shape[dim], axis=dim)
        below = lax.ppermute(tail, axis, [(i, i + 1) for i in range(ends)])
        above = lax.ppermute(head, axis, [(i + 1, i) for i in range(ends)])
        out.append((below, above))
    return out


def shifted(v, dim, below, above):
    n = v.shape[dim]
    minus = jnp.concatenate([below, lax.slice_in_dim(v, 0, n - 1, axis=dim)], axis=dim)
    plus = jnp.concatenate([lax.slice_in_dim(v, 1, n, axis=dim), above], axis=dim)
    return minus, plus


def laplace_halo(v, halos, dims):
    total = None
    for (below, above), dim in zip(halos, dims):
        minus, plus = shifted(v, dim, below.astype(v.dtype), above.astype(v.dtype))
        pair = minus + plus
        total = pair if total is None else total + pair
    return total - 6.0 * v


def block_shift(v, dim, width):
    n = v.shape[dim]
    zero = jnp.zeros_like(lax.slice_in_dim(v, 0, 1, axis=dim))
    minus = jnp.concatenate([zero, lax.slice_in_dim(v, 0, n - 1, axis=dim)], axis=dim)
    plus = jnp.concatenate([lax.slice_in_dim(v, 1, n, axis=dim), zero], axis=dim)
    pos = lax.broadcasted_iota(jnp.int32, v.shape, dim) % width
    minus = jnp.where(pos == 0, 0.0, minus)
    plus = jnp.where(pos == width - 1, 0.0, plus)
    return minus + plus


def laplace_blocks(v):
    return block_shift(v, 1, BX) + block_shift(v, 2, BY) + block_shift(v, 3, BZ) - 6.0 * v


def couple(matrix, v):
    return jnp.sum(matrix[:, :, None, None, None] * v[None], axis=1)


def global_sum(x):
    if REDUCE == "psum":
        return lax.psum(x, ("gx", "gy", "gz"))
    if REDUCE == "exchange":
        for group in (("gy", "gz"), ("gx",)):
            count = 1
            for axis in group:
                count *= lax.axis_size(axis)
            spread = jnp.broadcast_to(x.reshape(1), (count,))
            x = jnp.sum(lax.all_to_all(spread, group, 0, 0, tiled=True))
        return x
    if REDUCE == "gather":
        every = lax.all_gather(x.reshape(1), ("gx", "gy", "gz"), tiled=True)
        return jnp.sum(every)
    for axis in ("gz", "gy", "gx"):
        n = lax.axis_size(axis)
        step = 1
        while step < n:
            x = x + lax.ppermute(x, axis, [(i, (i + step) % n) for i in range(n)])
            step *= 2
    return x


def to_cells(blocks):
    depth = blocks.shape[1]
    shaped = blocks.reshape(NBX, NBY, NBZ, depth, BX, BY, BZ)
    return shaped.transpose(3, 0, 4, 1, 5, 2, 6).reshape(depth, NBX * BX, NBY * BY, NBZ * BZ)


def per_block_cells(values):
    depth = values.shape[1]
    shaped = values.reshape(NBX, NBY, NBZ, depth).transpose(3, 0, 1, 2)
    shaped = jnp.broadcast_to(
        shaped[:, :, None, :, None, :, None], (depth, NBX, BX, NBY, BY, NBZ, BZ)
    )
    return shaped.reshape(depth, NBX * BX, NBY * BY, NBZ * BZ)


def block_sums(cells):
    depth = cells.shape[0]
    shaped = cells.reshape(depth, NBX, BX, NBY, BY, NBZ, BZ)
    return jnp.sum(shaped, axis=(0, 2, 4, 6)).reshape(NBX * NBY * NBZ)


def _masks(rows_n, lanes_n):
    rows = lax.broadcasted_iota(jnp.int32, (rows_n, lanes_n), 0)
    lanes = lax.broadcasted_iota(jnp.int32, (rows_n, lanes_n), 1)
    r_src = (pltpu.roll(rows, 1, 0), pltpu.roll(rows, rows_n - 1, 0))
    l_src = (pltpu.roll(lanes, 1, 1), pltpu.roll(lanes, lanes_n - 1, 1))
    return rows, lanes, r_src, l_src


def _rolled(v):
    rows_n, lanes_n = v.shape
    return (
        (pltpu.roll(v, 1, 0), pltpu.roll(v, rows_n - 1, 0)),
        (pltpu.roll(v, 1, 1), pltpu.roll(v, lanes_n - 1, 1)),
    )


def _lap_halo(c, xm, xp, ylo, yhi, zlo, zhi, geo):
    rows, lanes, r_src, l_src = geo
    rows_n, lanes_n = c.shape
    (r1, r2), (l1, l2) = _rolled(c)
    y_out = jnp.where(rows == 0, ylo, yhi)
    z_out = jnp.where(lanes == 0, zlo, zhi)
    t1 = jnp.where(jnp.abs(r_src[0] - rows) == 1, r1, y_out)
    t2 = jnp.where(jnp.abs(r_src[1] - rows) == 1, r2, y_out)
    u1 = jnp.where(jnp.abs(l_src[0] - lanes) == 1, l1, z_out)
    u2 = jnp.where(jnp.abs(l_src[1] - lanes) == 1, l2, z_out)
    return (xp + xm) + (t1 + t2) + (u1 + u2) - 6.0 * c


def _lap_block(c, partner_x, geo):
    rows, lanes, r_src, l_src = geo
    (r1, r2), (l1, l2) = _rolled(c)
    t1 = jnp.where(r_src[0] // BY == rows // BY, r1, 0.0)
    t2 = jnp.where(r_src[1] // BY == rows // BY, r2, 0.0)
    u1 = jnp.where(l_src[0] // BZ == lanes // BZ, l1, 0.0)
    u2 = jnp.where(l_src[1] // BZ == lanes // BZ, l2, 0.0)
    return partner_x + (t1 + t2) + (u1 + u2) - 6.0 * c


def _couple(c_ref, vals, transpose):
    out = []
    for f in range(len(vals)):
        def m(g):
            return c_ref[g, f] if transpose else c_ref[f, g]
        acc = m(0) * vals[0]
        for g in range(1, len(vals)):
            acc = acc + m(g) * vals[g]
        out.append(acc)
    return out


def primal_kernel(c_ref, s_ref, d_ref, xlo, xhi, ylo, yhi, zlo, zhi,
                  s1_ref, eff_ref, oxlo, oxhi, oylo, oyhi, ozlo, ozhi):
    nf, nx, ny, nz = s_ref.shape
    geo = _masks(ny, nz)
    f32 = jnp.float32
    s = [[s_ref[f, x].astype(f32) for x in range(nx)] for f in range(nf)]
    for x in range(nx):
        d = d_ref[x].astype(f32)
        col = [s[f][x] for f in range(nf)]
        cs = _couple(c_ref, col, False)
        s1 = []
        for f in range(nf):
            xm = s[f][x - 1] if x > 0 else xlo[f, 0].astype(f32)
            xp = s[f][x + 1] if x < nx - 1 else xhi[f, 0].astype(f32)
            lap = _lap_halo(s[f][x], xm, xp, ylo[f, x].astype(f32), yhi[f, x].astype(f32),
                            zlo[f, x].astype(f32), zhi[f, x].astype(f32), geo)
            v = s[f][x] + primal_step * (d * lap + cs[f])
            s1.append(v)
            s1_ref[f, x] = v
            low = v.astype(jnp.bfloat16)
            if x == 0:
                oxlo[f, 0] = low
            if x == nx - 1:
                oxhi[f, 0] = low
            oylo[f, x] = low[0:1, :]
            oyhi[f, x] = low[ny - 1:ny, :]
            ozlo[f, x] = low[:, 0:1]
            ozhi[f, x] = low[:, nz - 1:nz]
        eff_ref[x] = (d * (1.0 + 0.5 * jnp.tanh(s1[0]))).astype(jnp.bfloat16)


def adjoint_kernel(c_ref, s1_ref, s_ref, d_ref, xlo, xhi, ylo, yhi, zlo, zhi, eff_ref, goal_ref, react_ref,
                   enr_ref, part_ref):
    nf, nx, ny, nz = s_ref.shape
    geo = _masks(ny, nz)
    f32 = jnp.float32
    s1 = [[s1_ref[f, x] for x in range(nx)] for f in range(nf)]
    residual = [[None] * nx for _ in range(nf)]
    for x in range(nx):
        d = d_ref[x].astype(f32)
        cs = _couple(c_ref, [s1[f][x] for f in range(nf)], False)
        for f in range(nf):
            xm = s1[f][x - 1] if x > 0 else xlo[f, 0].astype(f32)
            xp = s1[f][x + 1] if x < nx - 1 else xhi[f, 0].astype(f32)
            lap = _lap_halo(s1[f][x], xm, xp, ylo[f, x].astype(f32), yhi[f, x].astype(f32),
                            zlo[f, x].astype(f32), zhi[f, x].astype(f32), geo)
            residual[f][x] = d * lap + cs[f] - (s1[f][x] - s_ref[f, x].astype(f32)) / primal_step
    eff = [eff_ref[x].astype(f32) for x in range(nx)]
    goal = [[goal_ref[f, x].astype(f32) for x in range(nx)] for f in range(nf)]
    react = [[react_ref[f, x].astype(f32) for x in range(nx)] for f in range(nf)]
    dual = [list(row) for row in goal]
    for _ in range(SECTIONS):
        new = [[None] * nx for _ in range(nf)]
        for x in range(nx):
            ct = _couple(c_ref, [dual[f][x] for f in range(nf)], True)
            for f in range(nf):
                lap = _lap_block(dual[f][x], dual[f][x ^ 1], geo)
                new[f][x] = dual[f][x] + dual_step * (
                    eff[x] * lap + ct[f] - react[f][x] * dual[f][x] + goal[f][x]
                )
        dual = new
    for bx in range(nx // BX):
        acc = None
        for x in range(bx * BX, bx * BX + BX):
            for f in range(nf):
                lap = _lap_block(dual[f][x], dual[f][x ^ 1], geo)
                e = (dual[f][x] + 0.125 * lap).astype(jnp.bfloat16)
                enr_ref[f, x] = e
                term = jnp.abs(residual[f][x] * e.astype(f32))
                acc = term if acc is None else acc + term
        part_ref[bx] = acc


def shards(state, diffusivity, coupling, owner, levels, mark_count, goal_weight, reaction):
    sides = (("gx", 1), ("gy", 2), ("gz", 3))
    dims = (1, 2, 3)

    slots = goal_weight.shape[0]
    cells = FIELDS * BX * BY * BZ
    packed = jnp.concatenate(
        [
            goal_weight.reshape(slots, cells),
            jnp.pad(reaction, ((0, 0), (0, BZ - FIELDS))),
        ],
        axis=1,
    )

    f32, bf16 = jnp.float32, jnp.bfloat16
    nf, nx, ny, nz = state.shape
    vmem = pl.BlockSpec(memory_space=pltpu.VMEM)
    smem = pl.BlockSpec(memory_space=pltpu.SMEM)
    face_shapes = [(nf, 1, ny, nz)] * 2 + [(nf, nx, 1, nz)] * 2 + [(nf, nx, ny, 1)] * 2
    state_halo = [h for pair in faces(state, sides) for h in pair]
    packed, *state_halo = lax.optimization_barrier((packed, *state_halo))
    arrived = lax.all_to_all(packed, ("gy", "gz"), 0, 0, tiled=True)
    primal = pl.pallas_call(
        primal_kernel,
        out_shape=[jax.ShapeDtypeStruct(state.shape, f32), jax.ShapeDtypeStruct((nx, ny, nz), bf16)]
        + [jax.ShapeDtypeStruct(shape, bf16) for shape in face_shapes],
        in_specs=[smem] + [vmem] * 8,
        out_specs=[vmem] * 8,
    )(coupling, state, diffusivity, *state_halo)
    section_one, effective = primal[0], primal[1]
    section_halo = []
    for (axis, _), low, high in zip(sides, primal[2::2], primal[3::2]):
        ends = lax.axis_size(axis) - 1
        section_halo.append(lax.ppermute(high, axis, [(i, i + 1) for i in range(ends)]))
        section_halo.append(lax.ppermute(low, axis, [(i + 1, i) for i in range(ends)]))

    targets = owner[:, 0]
    order = jnp.arange(targets.shape[0], dtype=jnp.int32)
    same = targets[:, None] == targets[None, :]
    before = order[None, :] < order[:, None]
    rank = jnp.sum((same & before).astype(jnp.int32), axis=1)
    capacity = goal_weight.shape[0] // (lax.axis_size("gy") * lax.axis_size("gz"))
    slot_of = targets * capacity + rank

    mine = arrived[slot_of]
    goal = to_cells(mine[:, :cells].reshape(-1, FIELDS, BX, BY, BZ))
    react = per_block_cells(mine[:, cells : cells + FIELDS])
    enriched, part = pl.pallas_call(
        adjoint_kernel,
        out_shape=[jax.ShapeDtypeStruct(state.shape, bf16), jax.ShapeDtypeStruct((nx // BX, ny, nz), f32)],
        in_specs=[smem] + [vmem] * 12,
        out_specs=[vmem] * 2,
    )(coupling, section_one, state, diffusivity, *section_halo, effective, goal, react)
    sums = jnp.sum(part.reshape(nx // BX, ny // BY, BY, nz // BZ, BZ), axis=(2, 4)).reshape(-1)

    weights = jnp.exp2(2.0 * levels.astype(jnp.float32))
    indicator = weights * sums
    overall = global_sum(jnp.sum(indicator))
    block_count = owner.shape[0] * lax.axis_size("gx") * lax.axis_size("gy") * lax.axis_size("gz")
    share = indicator * block_count / overall
    marked = jnp.minimum(1.0, mark_count[0].astype(jnp.float32) * indicator / overall)
    return (enriched, share, marked)


def solution(mesh):
    placed = (
        P(None, "gx", "gy", "gz"),
        P("gx", "gy", "gz"),
        P(),
        P(("gx", "gy", "gz"), None),
        P(("gx", "gy", "gz")),
        P(),
        P(("gx", "gy", "gz"), None, None, None, None),
        P(("gx", "gy", "gz"), None),
    )
    return jax.shard_map(
        shards,
        mesh=mesh,
        in_specs=placed,
        out_specs=(P(None, "gx", "gy", "gz"), P(("gx", "gy", "gz")), P(("gx", "gy", "gz"))),
        check_vma=False,
    )
```

```python
import jax
import jax.numpy as jnp
from jax import lax
from jax.experimental import pallas as pl
from jax.experimental.pallas import tpu as pltpu
from jax.sharding import PartitionSpec as P

BX = 2
BY = 2
BZ = 128
NBX = 2
NBY = 4
NBZ = 6
SECTIONS = 3
FIELDS = 5


primal_step = 0.05
dual_step = 0.05

REDUCE = "exchange"


def faces(cells, sides):
    out = []
    for axis, dim in sides:
        count = lax.axis_size(axis)
        ends = count - 1
        head = lax.slice_in_dim(cells, 0, 1, axis=dim)
        tail = lax.slice_in_dim(cells, cells.shape[dim] - 1, cells.shape[dim], axis=dim)
        below = lax.ppermute(tail, axis, [(i, i + 1) for i in range(ends)])
        above = lax.ppermute(head, axis, [(i + 1, i) for i in range(ends)])
        out.append((below, above))
    return out


def shifted(v, dim, below, above):
    n = v.shape[dim]
    minus = jnp.concatenate([below, lax.slice_in_dim(v, 0, n - 1, axis=dim)], axis=dim)
    plus = jnp.concatenate([lax.slice_in_dim(v, 1, n, axis=dim), above], axis=dim)
    return minus, plus


def laplace_halo(v, halos, dims):
    total = None
    for (below, above), dim in zip(halos, dims):
        minus, plus = shifted(v, dim, below.astype(v.dtype), above.astype(v.dtype))
        pair = minus + plus
        total = pair if total is None else total + pair
    return total - 6.0 * v


def block_shift(v, dim, width):
    n = v.shape[dim]
    zero = jnp.zeros_like(lax.slice_in_dim(v, 0, 1, axis=dim))
    minus = jnp.concatenate([zero, lax.slice_in_dim(v, 0, n - 1, axis=dim)], axis=dim)
    plus = jnp.concatenate([lax.slice_in_dim(v, 1, n, axis=dim), zero], axis=dim)
    pos = lax.broadcasted_iota(jnp.int32, v.shape, dim) % width
    minus = jnp.where(pos == 0, 0.0, minus)
    plus = jnp.where(pos == width - 1, 0.0, plus)
    return minus + plus


def laplace_blocks(v):
    return block_shift(v, 1, BX) + block_shift(v, 2, BY) + block_shift(v, 3, BZ) - 6.0 * v


def couple(matrix, v):
    return jnp.sum(matrix[:, :, None, None, None] * v[None], axis=1)


def global_sum(x):
    if REDUCE == "psum":
        return lax.psum(x, ("gx", "gy", "gz"))
    if REDUCE == "exchange":
        for group in (("gy", "gz"), ("gx",)):
            count = 1
            for axis in group:
                count *= lax.axis_size(axis)
            spread = jnp.broadcast_to(x.reshape(1), (count,))
            x = jnp.sum(lax.all_to_all(spread, group, 0, 0, tiled=True))
        return x
    if REDUCE == "gather":
        every = lax.all_gather(x.reshape(1), ("gx", "gy", "gz"), tiled=True)
        return jnp.sum(every)
    for axis in ("gz", "gy", "gx"):
        n = lax.axis_size(axis)
        step = 1
        while step < n:
            x = x + lax.ppermute(x, axis, [(i, (i + step) % n) for i in range(n)])
            step *= 2
    return x


def to_cells(blocks):
    depth = blocks.shape[1]
    shaped = blocks.reshape(NBX, NBY, NBZ, depth, BX, BY, BZ)
    return shaped.transpose(3, 0, 4, 1, 5, 2, 6).reshape(depth, NBX * BX, NBY * BY, NBZ * BZ)


def per_block_cells(values):
    depth = values.shape[1]
    shaped = values.reshape(NBX, NBY, NBZ, depth).transpose(3, 0, 1, 2)
    shaped = jnp.broadcast_to(
        shaped[:, :, None, :, None, :, None], (depth, NBX, BX, NBY, BY, NBZ, BZ)
    )
    return shaped.reshape(depth, NBX * BX, NBY * BY, NBZ * BZ)


def block_sums(cells):
    depth = cells.shape[0]
    shaped = cells.reshape(depth, NBX, BX, NBY, BY, NBZ, BZ)
    return jnp.sum(shaped, axis=(0, 2, 4, 6)).reshape(NBX * NBY * NBZ)


def _masks(rows_n, lanes_n):
    rows = lax.broadcasted_iota(jnp.int32, (rows_n, lanes_n), 0)
    lanes = lax.broadcasted_iota(jnp.int32, (rows_n, lanes_n), 1)
    r_src = (pltpu.roll(rows, 1, 0), pltpu.roll(rows, rows_n - 1, 0))
    l_src = (pltpu.roll(lanes, 1, 1), pltpu.roll(lanes, lanes_n - 1, 1))
    return rows, lanes, r_src, l_src


def _rolled(v):
    rows_n, lanes_n = v.shape
    return (
        (pltpu.roll(v, 1, 0), pltpu.roll(v, rows_n - 1, 0)),
        (pltpu.roll(v, 1, 1), pltpu.roll(v, lanes_n - 1, 1)),
    )


def _lap_halo(c, xm, xp, ylo, yhi, zlo, zhi, geo):
    rows, lanes, r_src, l_src = geo
    rows_n, lanes_n = c.shape
    (r1, r2), (l1, l2) = _rolled(c)
    y_out = jnp.where(rows == 0, ylo, yhi)
    z_out = jnp.where(lanes == 0, zlo, zhi)
    t1 = jnp.where(jnp.abs(r_src[0] - rows) == 1, r1, y_out)
    t2 = jnp.where(jnp.abs(r_src[1] - rows) == 1, r2, y_out)
    u1 = jnp.where(jnp.abs(l_src[0] - lanes) == 1, l1, z_out)
    u2 = jnp.where(jnp.abs(l_src[1] - lanes) == 1, l2, z_out)
    return (xp + xm) + (t1 + t2) + (u1 + u2) - 6.0 * c


def _lap_block(c, partner_x, geo):
    rows, lanes, r_src, l_src = geo
    (r1, r2), (l1, l2) = _rolled(c)
    t1 = jnp.where(r_src[0] // BY == rows // BY, r1, 0.0)
    t2 = jnp.where(r_src[1] // BY == rows // BY, r2, 0.0)
    u1 = jnp.where(l_src[0] // BZ == lanes // BZ, l1, 0.0)
    u2 = jnp.where(l_src[1] // BZ == lanes // BZ, l2, 0.0)
    return partner_x + (t1 + t2) + (u1 + u2) - 6.0 * c


def _couple(c_ref, vals, transpose):
    out = []
    for f in range(len(vals)):
        def m(g):
            return c_ref[g, f] if transpose else c_ref[f, g]
        acc = m(0) * vals[0]
        for g in range(1, len(vals)):
            acc = acc + m(g) * vals[g]
        out.append(acc)
    return out


def primal_kernel(c_ref, s_ref, d_ref, xlo, xhi, ylo, yhi, zlo, zhi,
                  s1_ref, eff_ref, oxlo, oxhi, oylo, oyhi, ozlo, ozhi):
    nf, nx, ny, nz = s_ref.shape
    geo = _masks(ny, nz)
    f32 = jnp.float32
    s = [[s_ref[f, x].astype(f32) for x in range(nx)] for f in range(nf)]
    for x in range(nx):
        d = d_ref[x].astype(f32)
        col = [s[f][x] for f in range(nf)]
        cs = _couple(c_ref, col, False)
        s1 = []
        for f in range(nf):
            xm = s[f][x - 1] if x > 0 else xlo[f, 0].astype(f32)
            xp = s[f][x + 1] if x < nx - 1 else xhi[f, 0].astype(f32)
            lap = _lap_halo(s[f][x], xm, xp, ylo[f, x].astype(f32), yhi[f, x].astype(f32),
                            zlo[f, x].astype(f32), zhi[f, x].astype(f32), geo)
            v = s[f][x] + primal_step * (d * lap + cs[f])
            s1.append(v)
            s1_ref[f, x] = v
            low = v.astype(jnp.bfloat16)
            if x == 0:
                oxlo[f, 0] = low
            if x == nx - 1:
                oxhi[f, 0] = low
            oylo[f, x] = low[0:1, :]
            oyhi[f, x] = low[ny - 1:ny, :]
            ozlo[f, x] = low[:, 0:1]
            ozhi[f, x] = low[:, nz - 1:nz]
        eff_ref[x] = (d * (1.0 + 0.5 * jnp.tanh(s1[0]))).astype(jnp.bfloat16)


def adjoint_kernel(c_ref, s1_ref, s_ref, d_ref, xlo, xhi, ylo, yhi, zlo, zhi, eff_ref, goal_ref, react_ref,
                   w_ref, enr_ref, part_ref, spread_ref):
    nf, nx, ny, nz = s_ref.shape
    geo = _masks(ny, nz)
    f32 = jnp.float32
    s1 = [[s1_ref[f, x] for x in range(nx)] for f in range(nf)]
    residual = [[None] * nx for _ in range(nf)]
    for x in range(nx):
        d = d_ref[x].astype(f32)
        cs = _couple(c_ref, [s1[f][x] for f in range(nf)], False)
        for f in range(nf):
            xm = s1[f][x - 1] if x > 0 else xlo[f, 0].astype(f32)
            xp = s1[f][x + 1] if x < nx - 1 else xhi[f, 0].astype(f32)
            lap = _lap_halo(s1[f][x], xm, xp, ylo[f, x].astype(f32), yhi[f, x].astype(f32),
                            zlo[f, x].astype(f32), zhi[f, x].astype(f32), geo)
            residual[f][x] = d * lap + cs[f] - (s1[f][x] - s_ref[f, x].astype(f32)) / primal_step
    eff = [eff_ref[x].astype(f32) for x in range(nx)]
    goal = [[goal_ref[f, x].astype(f32) for x in range(nx)] for f in range(nf)]
    react = [[react_ref[f, x].astype(f32) for x in range(nx)] for f in range(nf)]
    dual = [list(row) for row in goal]
    for _ in range(SECTIONS):
        new = [[None] * nx for _ in range(nf)]
        for x in range(nx):
            ct = _couple(c_ref, [dual[f][x] for f in range(nf)], True)
            for f in range(nf):
                lap = _lap_block(dual[f][x], dual[f][x ^ 1], geo)
                new[f][x] = dual[f][x] + dual_step * (
                    eff[x] * lap + ct[f] - react[f][x] * dual[f][x] + goal[f][x]
                )
        dual = new
    for bx in range(nx // BX):
        acc = None
        for x in range(bx * BX, bx * BX + BX):
            for f in range(nf):
                lap = _lap_block(dual[f][x], dual[f][x ^ 1], geo)
                e = (dual[f][x] + 0.125 * lap).astype(jnp.bfloat16)
                enr_ref[f, x] = e
                term = jnp.abs(residual[f][x] * e.astype(f32))
                acc = term if acc is None else acc + term
        part_ref[bx] = acc
        weighted = acc * w_ref[bx]
        total = weighted if bx == 0 else total + weighted
    total = jnp.sum(jnp.sum(total, axis=1, keepdims=True), axis=0, keepdims=True)
    spread_ref[...] = jnp.broadcast_to(total, spread_ref.shape)


def shards(state, diffusivity, coupling, owner, levels, mark_count, goal_weight, reaction):
    sides = (("gx", 1), ("gy", 2), ("gz", 3))
    dims = (1, 2, 3)

    slots = goal_weight.shape[0]
    cells = FIELDS * BX * BY * BZ
    packed = jnp.concatenate(
        [
            goal_weight.reshape(slots, cells),
            jnp.pad(reaction, ((0, 0), (0, BZ - FIELDS))),
        ],
        axis=1,
    )

    f32, bf16 = jnp.float32, jnp.bfloat16
    nf, nx, ny, nz = state.shape
    vmem = pl.BlockSpec(memory_space=pltpu.VMEM)
    smem = pl.BlockSpec(memory_space=pltpu.SMEM)
    face_shapes = [(nf, 1, ny, nz)] * 2 + [(nf, nx, 1, nz)] * 2 + [(nf, nx, ny, 1)] * 2
    state_halo = [h for pair in faces(state, sides) for h in pair]
    packed, *state_halo = lax.optimization_barrier((packed, *state_halo))
    arrived = lax.all_to_all(packed, ("gy", "gz"), 0, 0, tiled=True)
    primal = pl.pallas_call(
        primal_kernel,
        out_shape=[jax.ShapeDtypeStruct(state.shape, f32), jax.ShapeDtypeStruct((nx, ny, nz), bf16)]
        + [jax.ShapeDtypeStruct(shape, bf16) for shape in face_shapes],
        in_specs=[smem] + [vmem] * 8,
        out_specs=[vmem] * 8,
    )(coupling, state, diffusivity, *state_halo)
    section_one, effective = primal[0], primal[1]
    section_halo = []
    for (axis, _), low, high in zip(sides, primal[2::2], primal[3::2]):
        ends = lax.axis_size(axis) - 1
        section_halo.append(lax.ppermute(high, axis, [(i, i + 1) for i in range(ends)]))
        section_halo.append(lax.ppermute(low, axis, [(i + 1, i) for i in range(ends)]))

    targets = owner[:, 0]
    order = jnp.arange(targets.shape[0], dtype=jnp.int32)
    same = targets[:, None] == targets[None, :]
    before = order[None, :] < order[:, None]
    rank = jnp.sum((same & before).astype(jnp.int32), axis=1)
    capacity = goal_weight.shape[0] // (lax.axis_size("gy") * lax.axis_size("gz"))
    slot_of = targets * capacity + rank

    mine = arrived[slot_of]
    goal = to_cells(mine[:, :cells].reshape(-1, FIELDS, BX, BY, BZ))
    react = per_block_cells(mine[:, cells : cells + FIELDS])
    weights = jnp.exp2(2.0 * levels.astype(jnp.float32))
    weight_cells = jnp.broadcast_to(
        weights.reshape(NBX, NBY, 1, NBZ, 1), (NBX, NBY, BY, NBZ, BZ)
    ).reshape(nx // BX, ny, nz)
    plane = lax.axis_size("gy") * lax.axis_size("gz")
    enriched, part, spread = pl.pallas_call(
        adjoint_kernel,
        out_shape=[
            jax.ShapeDtypeStruct(state.shape, bf16),
            jax.ShapeDtypeStruct((nx // BX, ny, nz), f32),
            jax.ShapeDtypeStruct((plane, 1), f32),
        ],
        in_specs=[smem] + [vmem] * 13,
        out_specs=[vmem] * 3,
    )(coupling, section_one, state, diffusivity, *section_halo, effective, goal, react, weight_cells)
    sums = jnp.sum(part.reshape(nx // BX, ny // BY, BY, nz // BZ, BZ), axis=(2, 4)).reshape(-1)
    indicator = weights * sums

    across = lax.axis_size("gx")
    level_one = lax.all_to_all(spread, ("gy", "gz"), 0, 0, tiled=True)
    level_two = lax.all_to_all(
        jnp.broadcast_to(level_one.reshape(1, plane), (across, plane)), ("gx",), 0, 0, tiled=True
    )
    overall = jnp.sum(level_two)
    block_count = owner.shape[0] * lax.axis_size("gx") * lax.axis_size("gy") * lax.axis_size("gz")
    share = indicator * block_count / overall
    marked = jnp.minimum(1.0, mark_count[0].astype(jnp.float32) * indicator / overall)
    return (enriched, share, marked)


def solution(mesh):
    placed = (
        P(None, "gx", "gy", "gz"),
        P("gx", "gy", "gz"),
        P(),
        P(("gx", "gy", "gz"), None),
        P(("gx", "gy", "gz")),
        P(),
        P(("gx", "gy", "gz"), None, None, None, None),
        P(("gx", "gy", "gz"), None),
    )
    return jax.shard_map(
        shards,
        mesh=mesh,
        in_specs=placed,
        out_specs=(P(None, "gx", "gy", "gz"), P(("gx", "gy", "gz")), P(("gx", "gy", "gz"))),
        check_vma=False,
    )
```

```python
import jax
import jax.numpy as jnp
from jax import lax
from jax.experimental import pallas as pl
from jax.experimental.pallas import tpu as pltpu
from jax.sharding import PartitionSpec as P

BX = 2
BY = 2
BZ = 128
NBX = 2
NBY = 4
NBZ = 6
SECTIONS = 3
FIELDS = 5


primal_step = 0.05
dual_step = 0.05

REDUCE = "exchange"


def faces(cells, sides):
    out = []
    for axis, dim in sides:
        count = lax.axis_size(axis)
        ends = count - 1
        head = lax.slice_in_dim(cells, 0, 1, axis=dim)
        tail = lax.slice_in_dim(cells, cells.shape[dim] - 1, cells.shape[dim], axis=dim)
        below = lax.ppermute(tail, axis, [(i, i + 1) for i in range(ends)])
        above = lax.ppermute(head, axis, [(i + 1, i) for i in range(ends)])
        out.append((below, above))
    return out


def shifted(v, dim, below, above):
    n = v.shape[dim]
    minus = jnp.concatenate([below, lax.slice_in_dim(v, 0, n - 1, axis=dim)], axis=dim)
    plus = jnp.concatenate([lax.slice_in_dim(v, 1, n, axis=dim), above], axis=dim)
    return minus, plus


def laplace_halo(v, halos, dims):
    total = None
    for (below, above), dim in zip(halos, dims):
        minus, plus = shifted(v, dim, below.astype(v.dtype), above.astype(v.dtype))
        pair = minus + plus
        total = pair if total is None else total + pair
    return total - 6.0 * v


def block_shift(v, dim, width):
    n = v.shape[dim]
    zero = jnp.zeros_like(lax.slice_in_dim(v, 0, 1, axis=dim))
    minus = jnp.concatenate([zero, lax.slice_in_dim(v, 0, n - 1, axis=dim)], axis=dim)
    plus = jnp.concatenate([lax.slice_in_dim(v, 1, n, axis=dim), zero], axis=dim)
    pos = lax.broadcasted_iota(jnp.int32, v.shape, dim) % width
    minus = jnp.where(pos == 0, 0.0, minus)
    plus = jnp.where(pos == width - 1, 0.0, plus)
    return minus + plus


def laplace_blocks(v):
    return block_shift(v, 1, BX) + block_shift(v, 2, BY) + block_shift(v, 3, BZ) - 6.0 * v


def couple(matrix, v):
    return jnp.sum(matrix[:, :, None, None, None] * v[None], axis=1)


def global_sum(x):
    if REDUCE == "psum":
        return lax.psum(x, ("gx", "gy", "gz"))
    if REDUCE == "exchange":
        for group in (("gy", "gz"), ("gx",)):
            count = 1
            for axis in group:
                count *= lax.axis_size(axis)
            spread = jnp.broadcast_to(x.reshape(1), (count,))
            x = jnp.sum(lax.all_to_all(spread, group, 0, 0, tiled=True))
        return x
    if REDUCE == "gather":
        every = lax.all_gather(x.reshape(1), ("gx", "gy", "gz"), tiled=True)
        return jnp.sum(every)
    for axis in ("gz", "gy", "gx"):
        n = lax.axis_size(axis)
        step = 1
        while step < n:
            x = x + lax.ppermute(x, axis, [(i, (i + step) % n) for i in range(n)])
            step *= 2
    return x


def to_cells(blocks):
    depth = blocks.shape[1]
    shaped = blocks.reshape(NBX, NBY, NBZ, depth, BX, BY, BZ)
    return shaped.transpose(3, 0, 4, 1, 5, 2, 6).reshape(depth, NBX * BX, NBY * BY, NBZ * BZ)


def per_block_cells(values):
    depth = values.shape[1]
    shaped = values.reshape(NBX, NBY, NBZ, depth).transpose(3, 0, 1, 2)
    shaped = jnp.broadcast_to(
        shaped[:, :, None, :, None, :, None], (depth, NBX, BX, NBY, BY, NBZ, BZ)
    )
    return shaped.reshape(depth, NBX * BX, NBY * BY, NBZ * BZ)


def block_sums(cells):
    depth = cells.shape[0]
    shaped = cells.reshape(depth, NBX, BX, NBY, BY, NBZ, BZ)
    return jnp.sum(shaped, axis=(0, 2, 4, 6)).reshape(NBX * NBY * NBZ)


def _masks(rows_n, lanes_n):
    rows = lax.broadcasted_iota(jnp.int32, (rows_n, lanes_n), 0)
    lanes = lax.broadcasted_iota(jnp.int32, (rows_n, lanes_n), 1)
    r_src = (pltpu.roll(rows, 1, 0), pltpu.roll(rows, rows_n - 1, 0))
    l_src = (pltpu.roll(lanes, 1, 1), pltpu.roll(lanes, lanes_n - 1, 1))
    return rows, lanes, r_src, l_src


def _rolled(v):
    rows_n, lanes_n = v.shape
    return (
        (pltpu.roll(v, 1, 0), pltpu.roll(v, rows_n - 1, 0)),
        (pltpu.roll(v, 1, 1), pltpu.roll(v, lanes_n - 1, 1)),
    )


def _lap_halo(c, xm, xp, ylo, yhi, zlo, zhi, geo):
    rows, lanes, r_src, l_src = geo
    rows_n, lanes_n = c.shape
    (r1, r2), (l1, l2) = _rolled(c)
    y_out = jnp.where(rows == 0, ylo, yhi)
    z_out = jnp.where(lanes == 0, zlo, zhi)
    t1 = jnp.where(jnp.abs(r_src[0] - rows) == 1, r1, y_out)
    t2 = jnp.where(jnp.abs(r_src[1] - rows) == 1, r2, y_out)
    u1 = jnp.where(jnp.abs(l_src[0] - lanes) == 1, l1, z_out)
    u2 = jnp.where(jnp.abs(l_src[1] - lanes) == 1, l2, z_out)
    return (xp + xm) + (t1 + t2) + (u1 + u2) - 6.0 * c


def _lap_block(c, partner_x, geo):
    rows, lanes, r_src, l_src = geo
    (r1, r2), (l1, l2) = _rolled(c)
    t1 = jnp.where(r_src[0] // BY == rows // BY, r1, 0.0)
    t2 = jnp.where(r_src[1] // BY == rows // BY, r2, 0.0)
    u1 = jnp.where(l_src[0] // BZ == lanes // BZ, l1, 0.0)
    u2 = jnp.where(l_src[1] // BZ == lanes // BZ, l2, 0.0)
    return partner_x + (t1 + t2) + (u1 + u2) - 6.0 * c


def _couple(c_ref, vals, transpose):
    out = []
    for f in range(len(vals)):
        def m(g):
            return c_ref[g, f] if transpose else c_ref[f, g]
        acc = m(0) * vals[0]
        for g in range(1, len(vals)):
            acc = acc + m(g) * vals[g]
        out.append(acc)
    return out


def primal_kernel(c_ref, s_ref, d_ref, xlo, xhi, ylo, yhi, zlo, zhi,
                  s1_ref, eff_ref, oxlo, oxhi, oylo, oyhi, ozlo, ozhi):
    nf, nx, ny, nz = s_ref.shape
    geo = _masks(ny, nz)
    f32 = jnp.float32
    s = [[s_ref[f, x].astype(f32) for x in range(nx)] for f in range(nf)]
    for x in range(nx):
        d = d_ref[x].astype(f32)
        col = [s[f][x] for f in range(nf)]
        cs = _couple(c_ref, col, False)
        s1 = []
        for f in range(nf):
            xm = s[f][x - 1] if x > 0 else xlo[f, 0].astype(f32)
            xp = s[f][x + 1] if x < nx - 1 else xhi[f, 0].astype(f32)
            lap = _lap_halo(s[f][x], xm, xp, ylo[f, x].astype(f32), yhi[f, x].astype(f32),
                            zlo[f, x].astype(f32), zhi[f, x].astype(f32), geo)
            v = s[f][x] + primal_step * (d * lap + cs[f])
            s1.append(v)
            s1_ref[f, x] = v
            low = v.astype(jnp.bfloat16)
            if x == 0:
                oxlo[f, 0] = low
            if x == nx - 1:
                oxhi[f, 0] = low
            oylo[f, x] = low[0:1, :]
            oyhi[f, x] = low[ny - 1:ny, :]
            ozlo[f, x] = low[:, 0:1]
            ozhi[f, x] = low[:, nz - 1:nz]
        eff_ref[x] = (d * (1.0 + 0.5 * jnp.tanh(s1[0]))).astype(jnp.bfloat16)


def adjoint_kernel(c_ref, slot_ref, s1_ref, s_ref, d_ref, xlo, xhi, ylo, yhi, zlo, zhi, eff_ref, arr_ref,
                   w_ref, enr_ref, part_ref, spread_ref, goal_ref, react_ref):
    nf, nx, ny, nz = s_ref.shape
    geo = _masks(ny, nz)
    f32 = jnp.float32
    s1 = [[s1_ref[f, x] for x in range(nx)] for f in range(nf)]
    residual = [[None] * nx for _ in range(nf)]
    for x in range(nx):
        d = d_ref[x].astype(f32)
        cs = _couple(c_ref, [s1[f][x] for f in range(nf)], False)
        for f in range(nf):
            xm = s1[f][x - 1] if x > 0 else xlo[f, 0].astype(f32)
            xp = s1[f][x + 1] if x < nx - 1 else xhi[f, 0].astype(f32)
            lap = _lap_halo(s1[f][x], xm, xp, ylo[f, x].astype(f32), yhi[f, x].astype(f32),
                            zlo[f, x].astype(f32), zhi[f, x].astype(f32), geo)
            residual[f][x] = d * lap + cs[f] - (s1[f][x] - s_ref[f, x].astype(f32)) / primal_step
    for b in range(NBX * NBY * NBZ):
        bx, by, bz = b // (NBY * NBZ), (b // NBZ) % NBY, b % NBZ
        rows = arr_ref[slot_ref[b]].astype(f32)
        lanes = pl.ds(bz * BZ, BZ)
        for f in range(nf):
            rate = jnp.broadcast_to(rows[nf * BX * BY:nf * BX * BY + 1, f:f + 1], (1, BZ))
            for i in range(BX):
                for j in range(BY):
                    r = (f * BX + i) * BY + j
                    y = pl.ds(by * BY + j, 1)
                    goal_ref[f, bx * BX + i, y, lanes] = rows[r:r + 1, :]
                    react_ref[f, bx * BX + i, y, lanes] = rate
    eff = [eff_ref[x].astype(f32) for x in range(nx)]
    goal = [[goal_ref[f, x] for x in range(nx)] for f in range(nf)]
    react = [[react_ref[f, x] for x in range(nx)] for f in range(nf)]
    dual = [list(row) for row in goal]
    for _ in range(SECTIONS):
        new = [[None] * nx for _ in range(nf)]
        for x in range(nx):
            ct = _couple(c_ref, [dual[f][x] for f in range(nf)], True)
            for f in range(nf):
                lap = _lap_block(dual[f][x], dual[f][x ^ 1], geo)
                new[f][x] = dual[f][x] + dual_step * (
                    eff[x] * lap + ct[f] - react[f][x] * dual[f][x] + goal[f][x]
                )
        dual = new
    for bx in range(nx // BX):
        acc = None
        for x in range(bx * BX, bx * BX + BX):
            for f in range(nf):
                lap = _lap_block(dual[f][x], dual[f][x ^ 1], geo)
                e = (dual[f][x] + 0.125 * lap).astype(jnp.bfloat16)
                enr_ref[f, x] = e
                term = jnp.abs(residual[f][x] * e.astype(f32))
                acc = term if acc is None else acc + term
        part_ref[bx] = acc
        weighted = acc * w_ref[bx]
        total = weighted if bx == 0 else total + weighted
    total = jnp.sum(jnp.sum(total, axis=1, keepdims=True), axis=0, keepdims=True)
    spread_ref[...] = jnp.broadcast_to(total, spread_ref.shape)


def shards(state, diffusivity, coupling, owner, levels, mark_count, goal_weight, reaction):
    sides = (("gx", 1), ("gy", 2), ("gz", 3))
    dims = (1, 2, 3)

    slots = goal_weight.shape[0]
    packed = jnp.concatenate(
        [
            goal_weight.reshape(slots, FIELDS * BX * BY, BZ),
            jnp.pad(reaction, ((0, 0), (0, BZ - FIELDS)))[:, None, :],
        ],
        axis=1,
    )

    f32, bf16 = jnp.float32, jnp.bfloat16
    nf, nx, ny, nz = state.shape
    vmem = pl.BlockSpec(memory_space=pltpu.VMEM)
    smem = pl.BlockSpec(memory_space=pltpu.SMEM)
    face_shapes = [(nf, 1, ny, nz)] * 2 + [(nf, nx, 1, nz)] * 2 + [(nf, nx, ny, 1)] * 2
    state_halo = [h for pair in faces(state, sides) for h in pair]
    packed, *state_halo = lax.optimization_barrier((packed, *state_halo))
    arrived = lax.all_to_all(packed, ("gy", "gz"), 0, 0, tiled=True)
    primal = pl.pallas_call(
        primal_kernel,
        out_shape=[jax.ShapeDtypeStruct(state.shape, f32), jax.ShapeDtypeStruct((nx, ny, nz), bf16)]
        + [jax.ShapeDtypeStruct(shape, bf16) for shape in face_shapes],
        in_specs=[smem] + [vmem] * 8,
        out_specs=[vmem] * 8,
    )(coupling, state, diffusivity, *state_halo)
    section_one, effective = primal[0], primal[1]
    section_halo = []
    for (axis, _), low, high in zip(sides, primal[2::2], primal[3::2]):
        ends = lax.axis_size(axis) - 1
        section_halo.append(lax.ppermute(high, axis, [(i, i + 1) for i in range(ends)]))
        section_halo.append(lax.ppermute(low, axis, [(i + 1, i) for i in range(ends)]))

    targets = owner[:, 0]
    order = jnp.arange(targets.shape[0], dtype=jnp.int32)
    same = targets[:, None] == targets[None, :]
    before = order[None, :] < order[:, None]
    rank = jnp.sum((same & before).astype(jnp.int32), axis=1)
    capacity = goal_weight.shape[0] // (lax.axis_size("gy") * lax.axis_size("gz"))
    slot_of = targets * capacity + rank

    weights = jnp.exp2(2.0 * levels.astype(jnp.float32))
    weight_cells = jnp.broadcast_to(
        weights.reshape(NBX, NBY, 1, NBZ, 1), (NBX, NBY, BY, NBZ, BZ)
    ).reshape(nx // BX, ny, nz)
    plane = lax.axis_size("gy") * lax.axis_size("gz")
    enriched, part, spread = pl.pallas_call(
        adjoint_kernel,
        out_shape=[
            jax.ShapeDtypeStruct(state.shape, bf16),
            jax.ShapeDtypeStruct((nx // BX, ny, nz), f32),
            jax.ShapeDtypeStruct((plane, 1), f32),
        ],
        in_specs=[smem, smem] + [vmem] * 12,
        out_specs=[vmem] * 3,
        scratch_shapes=[pltpu.VMEM(state.shape, f32), pltpu.VMEM(state.shape, f32)],
    )(coupling, slot_of, section_one, state, diffusivity, *section_halo, effective, arrived, weight_cells)
    sums = jnp.sum(part.reshape(nx // BX, ny // BY, BY, nz // BZ, BZ), axis=(2, 4)).reshape(-1)
    indicator = weights * sums

    across = lax.axis_size("gx")
    level_one = lax.all_to_all(spread, ("gy", "gz"), 0, 0, tiled=True)
    level_two = lax.all_to_all(
        jnp.broadcast_to(level_one.reshape(1, plane), (across, plane)), ("gx",), 0, 0, tiled=True
    )
    overall = jnp.sum(level_two)
    block_count = owner.shape[0] * lax.axis_size("gx") * lax.axis_size("gy") * lax.axis_size("gz")
    share = indicator * block_count / overall
    marked = jnp.minimum(1.0, mark_count[0].astype(jnp.float32) * indicator / overall)
    return (enriched, share, marked)


def solution(mesh):
    placed = (
        P(None, "gx", "gy", "gz"),
        P("gx", "gy", "gz"),
        P(),
        P(("gx", "gy", "gz"), None),
        P(("gx", "gy", "gz")),
        P(),
        P(("gx", "gy", "gz"), None, None, None, None),
        P(("gx", "gy", "gz"), None),
    )
    return jax.shard_map(
        shards,
        mesh=mesh,
        in_specs=placed,
        out_specs=(P(None, "gx", "gy", "gz"), P(("gx", "gy", "gz")), P(("gx", "gy", "gz"))),
        check_vma=False,
    )
```

```python
import jax
import jax.numpy as jnp
from jax import lax
from jax.experimental import pallas as pl
from jax.experimental.pallas import tpu as pltpu
from jax.sharding import PartitionSpec as P

BX = 2
BY = 2
BZ = 128
NBX = 2
NBY = 4
NBZ = 6
SECTIONS = 3
FIELDS = 5


primal_step = 0.05
dual_step = 0.05

REDUCE = "exchange"


def faces(cells, sides):
    out = []
    for axis, dim in sides:
        count = lax.axis_size(axis)
        ends = count - 1
        head = lax.slice_in_dim(cells, 0, 1, axis=dim)
        tail = lax.slice_in_dim(cells, cells.shape[dim] - 1, cells.shape[dim], axis=dim)
        below = lax.ppermute(tail, axis, [(i, i + 1) for i in range(ends)])
        above = lax.ppermute(head, axis, [(i + 1, i) for i in range(ends)])
        out.append((below, above))
    return out


def shifted(v, dim, below, above):
    n = v.shape[dim]
    minus = jnp.concatenate([below, lax.slice_in_dim(v, 0, n - 1, axis=dim)], axis=dim)
    plus = jnp.concatenate([lax.slice_in_dim(v, 1, n, axis=dim), above], axis=dim)
    return minus, plus


def laplace_halo(v, halos, dims):
    total = None
    for (below, above), dim in zip(halos, dims):
        minus, plus = shifted(v, dim, below.astype(v.dtype), above.astype(v.dtype))
        pair = minus + plus
        total = pair if total is None else total + pair
    return total - 6.0 * v


def block_shift(v, dim, width):
    n = v.shape[dim]
    zero = jnp.zeros_like(lax.slice_in_dim(v, 0, 1, axis=dim))
    minus = jnp.concatenate([zero, lax.slice_in_dim(v, 0, n - 1, axis=dim)], axis=dim)
    plus = jnp.concatenate([lax.slice_in_dim(v, 1, n, axis=dim), zero], axis=dim)
    pos = lax.broadcasted_iota(jnp.int32, v.shape, dim) % width
    minus = jnp.where(pos == 0, 0.0, minus)
    plus = jnp.where(pos == width - 1, 0.0, plus)
    return minus + plus


def laplace_blocks(v):
    return block_shift(v, 1, BX) + block_shift(v, 2, BY) + block_shift(v, 3, BZ) - 6.0 * v


def couple(matrix, v):
    return jnp.sum(matrix[:, :, None, None, None] * v[None], axis=1)


def global_sum(x):
    if REDUCE == "psum":
        return lax.psum(x, ("gx", "gy", "gz"))
    if REDUCE == "exchange":
        for group in (("gy", "gz"), ("gx",)):
            count = 1
            for axis in group:
                count *= lax.axis_size(axis)
            spread = jnp.broadcast_to(x.reshape(1), (count,))
            x = jnp.sum(lax.all_to_all(spread, group, 0, 0, tiled=True))
        return x
    if REDUCE == "gather":
        every = lax.all_gather(x.reshape(1), ("gx", "gy", "gz"), tiled=True)
        return jnp.sum(every)
    for axis in ("gz", "gy", "gx"):
        n = lax.axis_size(axis)
        step = 1
        while step < n:
            x = x + lax.ppermute(x, axis, [(i, (i + step) % n) for i in range(n)])
            step *= 2
    return x


def to_cells(blocks):
    depth = blocks.shape[1]
    shaped = blocks.reshape(NBX, NBY, NBZ, depth, BX, BY, BZ)
    return shaped.transpose(3, 0, 4, 1, 5, 2, 6).reshape(depth, NBX * BX, NBY * BY, NBZ * BZ)


def per_block_cells(values):
    depth = values.shape[1]
    shaped = values.reshape(NBX, NBY, NBZ, depth).transpose(3, 0, 1, 2)
    shaped = jnp.broadcast_to(
        shaped[:, :, None, :, None, :, None], (depth, NBX, BX, NBY, BY, NBZ, BZ)
    )
    return shaped.reshape(depth, NBX * BX, NBY * BY, NBZ * BZ)


def block_sums(cells):
    depth = cells.shape[0]
    shaped = cells.reshape(depth, NBX, BX, NBY, BY, NBZ, BZ)
    return jnp.sum(shaped, axis=(0, 2, 4, 6)).reshape(NBX * NBY * NBZ)


def _masks(rows_n, lanes_n):
    rows = lax.broadcasted_iota(jnp.int32, (rows_n, lanes_n), 0)
    lanes = lax.broadcasted_iota(jnp.int32, (rows_n, lanes_n), 1)
    r_src = (pltpu.roll(rows, 1, 0), pltpu.roll(rows, rows_n - 1, 0))
    l_src = (pltpu.roll(lanes, 1, 1), pltpu.roll(lanes, lanes_n - 1, 1))
    return rows, lanes, r_src, l_src


def _rolled(v):
    rows_n, lanes_n = v.shape
    return (
        (pltpu.roll(v, 1, 0), pltpu.roll(v, rows_n - 1, 0)),
        (pltpu.roll(v, 1, 1), pltpu.roll(v, lanes_n - 1, 1)),
    )


def _lap_halo(c, xm, xp, ylo, yhi, zlo, zhi, geo):
    rows, lanes, r_src, l_src = geo
    rows_n, lanes_n = c.shape
    (r1, r2), (l1, l2) = _rolled(c)
    y_out = jnp.where(rows == 0, ylo, yhi)
    z_out = jnp.where(lanes == 0, zlo, zhi)
    t1 = jnp.where(jnp.abs(r_src[0] - rows) == 1, r1, y_out)
    t2 = jnp.where(jnp.abs(r_src[1] - rows) == 1, r2, y_out)
    u1 = jnp.where(jnp.abs(l_src[0] - lanes) == 1, l1, z_out)
    u2 = jnp.where(jnp.abs(l_src[1] - lanes) == 1, l2, z_out)
    return (xp + xm) + (t1 + t2) + (u1 + u2) - 6.0 * c


def _lap_block(c, partner_x, geo):
    rows, lanes, r_src, l_src = geo
    (r1, r2), (l1, l2) = _rolled(c)
    t1 = jnp.where(r_src[0] // BY == rows // BY, r1, 0.0)
    t2 = jnp.where(r_src[1] // BY == rows // BY, r2, 0.0)
    u1 = jnp.where(l_src[0] // BZ == lanes // BZ, l1, 0.0)
    u2 = jnp.where(l_src[1] // BZ == lanes // BZ, l2, 0.0)
    return partner_x + (t1 + t2) + (u1 + u2) - 6.0 * c


def _couple(c_ref, vals, transpose):
    out = []
    for f in range(len(vals)):
        def m(g):
            return c_ref[g, f] if transpose else c_ref[f, g]
        acc = m(0) * vals[0]
        for g in range(1, len(vals)):
            acc = acc + m(g) * vals[g]
        out.append(acc)
    return out


def primal_kernel(c_ref, s_ref, d_ref, xlo, xhi, ylo, yhi, zlo, zhi,
                  s1_ref, eff_ref, oxlo, oxhi, oylo, oyhi, ozlo, ozhi):
    nf, nx, ny, nz = s_ref.shape
    geo = _masks(ny, nz)
    f32 = jnp.float32
    s = [[s_ref[f, x].astype(f32) for x in range(nx)] for f in range(nf)]
    for x in range(nx):
        d = d_ref[x].astype(f32)
        col = [s[f][x] for f in range(nf)]
        cs = _couple(c_ref, col, False)
        s1 = []
        for f in range(nf):
            xm = s[f][x - 1] if x > 0 else xlo[f, 0].astype(f32)
            xp = s[f][x + 1] if x < nx - 1 else xhi[f, 0].astype(f32)
            lap = _lap_halo(s[f][x], xm, xp, ylo[f, x].astype(f32), yhi[f, x].astype(f32),
                            zlo[f, x].astype(f32), zhi[f, x].astype(f32), geo)
            v = s[f][x] + primal_step * (d * lap + cs[f])
            s1.append(v)
            s1_ref[f, x] = v
            low = v.astype(jnp.bfloat16)
            if x == 0:
                oxlo[f, 0] = low
            if x == nx - 1:
                oxhi[f, 0] = low
            oylo[f, x] = low[0:1, :]
            oyhi[f, x] = low[ny - 1:ny, :]
            ozlo[f, x] = low[:, 0:1]
            ozhi[f, x] = low[:, nz - 1:nz]
        eff_ref[x] = (d * (1.0 + 0.5 * jnp.tanh(s1[0]))).astype(jnp.bfloat16)


def adjoint_kernel(c_ref, slot_ref, s1_ref, s_ref, d_ref, xlo, xhi, ylo, yhi, zlo, zhi, eff_ref, arr_ref,
                   w_ref, enr_ref, part_ref, spread_ref, goal_ref, react_ref):
    nf, nx, ny, nz = s_ref.shape
    geo = _masks(ny, nz)
    f32 = jnp.float32
    s1 = [[s1_ref[f, x] for x in range(nx)] for f in range(nf)]
    residual = [[None] * nx for _ in range(nf)]
    for x in range(nx):
        d = d_ref[x].astype(f32)
        cs = _couple(c_ref, [s1[f][x] for f in range(nf)], False)
        for f in range(nf):
            xm = s1[f][x - 1] if x > 0 else xlo[f, 0].astype(f32)
            xp = s1[f][x + 1] if x < nx - 1 else xhi[f, 0].astype(f32)
            lap = _lap_halo(s1[f][x], xm, xp, ylo[f, x].astype(f32), yhi[f, x].astype(f32),
                            zlo[f, x].astype(f32), zhi[f, x].astype(f32), geo)
            residual[f][x] = d * lap + cs[f] - (s1[f][x] - s_ref[f, x].astype(f32)) / primal_step
    for b in range(NBX * NBY * NBZ):
        bx, by, bz = b // (NBY * NBZ), (b // NBZ) % NBY, b % NBZ
        rows = arr_ref[slot_ref[b]].astype(f32)
        lanes = pl.ds(bz * BZ, BZ)
        for f in range(nf):
            rate = jnp.broadcast_to(rows[nf * BX * BY:nf * BX * BY + 1, f:f + 1], (1, BZ))
            for i in range(BX):
                for j in range(BY):
                    r = (f * BX + i) * BY + j
                    y = pl.ds(by * BY + j, 1)
                    goal_ref[f, bx * BX + i, y, lanes] = rows[r:r + 1, :]
                    react_ref[f, bx * BX + i, y, lanes] = rate
    eff = [eff_ref[x].astype(f32) for x in range(nx)]
    goal = [[goal_ref[f, x] for x in range(nx)] for f in range(nf)]
    react = [[react_ref[f, x] for x in range(nx)] for f in range(nf)]
    dual = [list(row) for row in goal]
    for _ in range(SECTIONS):
        new = [[None] * nx for _ in range(nf)]
        for x in range(nx):
            ct = _couple(c_ref, [dual[f][x] for f in range(nf)], True)
            for f in range(nf):
                lap = _lap_block(dual[f][x], dual[f][x ^ 1], geo)
                new[f][x] = dual[f][x] + dual_step * (
                    eff[x] * lap + ct[f] - react[f][x] * dual[f][x] + goal[f][x]
                )
        dual = new
    for bx in range(nx // BX):
        acc = None
        for x in range(bx * BX, bx * BX + BX):
            for f in range(nf):
                lap = _lap_block(dual[f][x], dual[f][x ^ 1], geo)
                e = (dual[f][x] + 0.125 * lap).astype(jnp.bfloat16)
                enr_ref[f, x] = e
                term = jnp.abs(residual[f][x] * e.astype(f32))
                acc = term if acc is None else acc + term
        part_ref[bx] = acc
        weighted = acc * w_ref[bx]
        total = weighted if bx == 0 else total + weighted
    total = jnp.sum(jnp.sum(total, axis=1, keepdims=True), axis=0, keepdims=True)
    spread_ref[...] = jnp.broadcast_to(total, spread_ref.shape)


def shards(state, diffusivity, coupling, owner, levels, mark_count, goal_weight, reaction):
    sides = (("gx", 1), ("gy", 2), ("gz", 3))
    dims = (1, 2, 3)

    slots = goal_weight.shape[0]
    packed = jnp.concatenate(
        [
            goal_weight.reshape(slots, FIELDS * BX * BY, BZ),
            jnp.pad(reaction, ((0, 0), (0, BZ - FIELDS)))[:, None, :],
        ],
        axis=1,
    )

    f32, bf16 = jnp.float32, jnp.bfloat16
    nf, nx, ny, nz = state.shape
    vmem = pl.BlockSpec(memory_space=pltpu.VMEM)
    smem = pl.BlockSpec(memory_space=pltpu.SMEM)
    face_shapes = [(nf, 1, ny, nz)] * 2 + [(nf, nx, 1, nz)] * 2 + [(nf, nx, ny, 1)] * 2
    state_halo = [h for pair in faces(state, sides) for h in pair]
    arrived = lax.all_to_all(packed, ("gy", "gz"), 0, 0, tiled=True)
    primal = pl.pallas_call(
        primal_kernel,
        out_shape=[jax.ShapeDtypeStruct(state.shape, f32), jax.ShapeDtypeStruct((nx, ny, nz), bf16)]
        + [jax.ShapeDtypeStruct(shape, bf16) for shape in face_shapes],
        in_specs=[smem] + [vmem] * 8,
        out_specs=[vmem] * 8,
    )(coupling, state, diffusivity, *state_halo)
    section_one, effective = primal[0], primal[1]
    section_halo = []
    for (axis, _), low, high in zip(sides, primal[2::2], primal[3::2]):
        ends = lax.axis_size(axis) - 1
        section_halo.append(lax.ppermute(high, axis, [(i, i + 1) for i in range(ends)]))
        section_halo.append(lax.ppermute(low, axis, [(i + 1, i) for i in range(ends)]))

    targets = owner[:, 0]
    order = jnp.arange(targets.shape[0], dtype=jnp.int32)
    same = targets[:, None] == targets[None, :]
    before = order[None, :] < order[:, None]
    rank = jnp.sum((same & before).astype(jnp.int32), axis=1)
    capacity = goal_weight.shape[0] // (lax.axis_size("gy") * lax.axis_size("gz"))
    slot_of = targets * capacity + rank

    weights = jnp.exp2(2.0 * levels.astype(jnp.float32))
    weight_cells = jnp.broadcast_to(
        weights.reshape(NBX, NBY, 1, NBZ, 1), (NBX, NBY, BY, NBZ, BZ)
    ).reshape(nx // BX, ny, nz)
    plane = lax.axis_size("gy") * lax.axis_size("gz")
    enriched, part, spread = pl.pallas_call(
        adjoint_kernel,
        out_shape=[
            jax.ShapeDtypeStruct(state.shape, bf16),
            jax.ShapeDtypeStruct((nx // BX, ny, nz), f32),
            jax.ShapeDtypeStruct((plane, 1), f32),
        ],
        in_specs=[smem, smem] + [vmem] * 12,
        out_specs=[vmem] * 3,
        scratch_shapes=[pltpu.VMEM(state.shape, f32), pltpu.VMEM(state.shape, f32)],
    )(coupling, slot_of, section_one, state, diffusivity, *section_halo, effective, arrived, weight_cells)
    sums = jnp.sum(part.reshape(nx // BX, ny // BY, BY, nz // BZ, BZ), axis=(2, 4)).reshape(-1)
    indicator = weights * sums

    across = lax.axis_size("gx")
    level_one = lax.all_to_all(spread, ("gy", "gz"), 0, 0, tiled=True)
    level_two = lax.all_to_all(
        jnp.broadcast_to(level_one.reshape(1, plane), (across, plane)), ("gx",), 0, 0, tiled=True
    )
    overall = jnp.sum(level_two)
    block_count = owner.shape[0] * lax.axis_size("gx") * lax.axis_size("gy") * lax.axis_size("gz")
    share = indicator * block_count / overall
    marked = jnp.minimum(1.0, mark_count[0].astype(jnp.float32) * indicator / overall)
    return (enriched, share, marked)


def solution(mesh):
    placed = (
        P(None, "gx", "gy", "gz"),
        P("gx", "gy", "gz"),
        P(),
        P(("gx", "gy", "gz"), None),
        P(("gx", "gy", "gz")),
        P(),
        P(("gx", "gy", "gz"), None, None, None, None),
        P(("gx", "gy", "gz"), None),
    )
    return jax.shard_map(
        shards,
        mesh=mesh,
        in_specs=placed,
        out_specs=(P(None, "gx", "gy", "gz"), P(("gx", "gy", "gz")), P(("gx", "gy", "gz"))),
        check_vma=False,
    )
```

```python
import jax
import jax.numpy as jnp
from jax import lax
from jax.experimental import pallas as pl
from jax.experimental.pallas import tpu as pltpu
from jax.sharding import PartitionSpec as P

BX = 2
BY = 2
BZ = 128
NBX = 2
NBY = 4
NBZ = 6
SECTIONS = 3
FIELDS = 5


primal_step = 0.05
dual_step = 0.05

REDUCE = "exchange"


def faces(cells, sides):
    out = []
    for axis, dim in sides:
        count = lax.axis_size(axis)
        ends = count - 1
        head = lax.slice_in_dim(cells, 0, 1, axis=dim)
        tail = lax.slice_in_dim(cells, cells.shape[dim] - 1, cells.shape[dim], axis=dim)
        below = lax.ppermute(tail, axis, [(i, i + 1) for i in range(ends)])
        above = lax.ppermute(head, axis, [(i + 1, i) for i in range(ends)])
        out.append((below, above))
    return out


def shifted(v, dim, below, above):
    n = v.shape[dim]
    minus = jnp.concatenate([below, lax.slice_in_dim(v, 0, n - 1, axis=dim)], axis=dim)
    plus = jnp.concatenate([lax.slice_in_dim(v, 1, n, axis=dim), above], axis=dim)
    return minus, plus


def laplace_halo(v, halos, dims):
    total = None
    for (below, above), dim in zip(halos, dims):
        minus, plus = shifted(v, dim, below.astype(v.dtype), above.astype(v.dtype))
        pair = minus + plus
        total = pair if total is None else total + pair
    return total - 6.0 * v


def block_shift(v, dim, width):
    n = v.shape[dim]
    zero = jnp.zeros_like(lax.slice_in_dim(v, 0, 1, axis=dim))
    minus = jnp.concatenate([zero, lax.slice_in_dim(v, 0, n - 1, axis=dim)], axis=dim)
    plus = jnp.concatenate([lax.slice_in_dim(v, 1, n, axis=dim), zero], axis=dim)
    pos = lax.broadcasted_iota(jnp.int32, v.shape, dim) % width
    minus = jnp.where(pos == 0, 0.0, minus)
    plus = jnp.where(pos == width - 1, 0.0, plus)
    return minus + plus


def laplace_blocks(v):
    return block_shift(v, 1, BX) + block_shift(v, 2, BY) + block_shift(v, 3, BZ) - 6.0 * v


def couple(matrix, v):
    return jnp.sum(matrix[:, :, None, None, None] * v[None], axis=1)


def global_sum(x):
    if REDUCE == "psum":
        return lax.psum(x, ("gx", "gy", "gz"))
    if REDUCE == "exchange":
        for group in (("gy", "gz"), ("gx",)):
            count = 1
            for axis in group:
                count *= lax.axis_size(axis)
            spread = jnp.broadcast_to(x.reshape(1), (count,))
            x = jnp.sum(lax.all_to_all(spread, group, 0, 0, tiled=True))
        return x
    if REDUCE == "gather":
        every = lax.all_gather(x.reshape(1), ("gx", "gy", "gz"), tiled=True)
        return jnp.sum(every)
    for axis in ("gz", "gy", "gx"):
        n = lax.axis_size(axis)
        step = 1
        while step < n:
            x = x + lax.ppermute(x, axis, [(i, (i + step) % n) for i in range(n)])
            step *= 2
    return x


def to_cells(blocks):
    depth = blocks.shape[1]
    shaped = blocks.reshape(NBX, NBY, NBZ, depth, BX, BY, BZ)
    return shaped.transpose(3, 0, 4, 1, 5, 2, 6).reshape(depth, NBX * BX, NBY * BY, NBZ * BZ)


def per_block_cells(values):
    depth = values.shape[1]
    shaped = values.reshape(NBX, NBY, NBZ, depth).transpose(3, 0, 1, 2)
    shaped = jnp.broadcast_to(
        shaped[:, :, None, :, None, :, None], (depth, NBX, BX, NBY, BY, NBZ, BZ)
    )
    return shaped.reshape(depth, NBX * BX, NBY * BY, NBZ * BZ)


def block_sums(cells):
    depth = cells.shape[0]
    shaped = cells.reshape(depth, NBX, BX, NBY, BY, NBZ, BZ)
    return jnp.sum(shaped, axis=(0, 2, 4, 6)).reshape(NBX * NBY * NBZ)


def _masks(rows_n, lanes_n):
    rows = lax.broadcasted_iota(jnp.int32, (rows_n, lanes_n), 0)
    lanes = lax.broadcasted_iota(jnp.int32, (rows_n, lanes_n), 1)
    r_src = (pltpu.roll(rows, 1, 0), pltpu.roll(rows, rows_n - 1, 0))
    l_src = (pltpu.roll(lanes, 1, 1), pltpu.roll(lanes, lanes_n - 1, 1))
    return rows, lanes, r_src, l_src


def _rolled(v):
    rows_n, lanes_n = v.shape
    return (
        (pltpu.roll(v, 1, 0), pltpu.roll(v, rows_n - 1, 0)),
        (pltpu.roll(v, 1, 1), pltpu.roll(v, lanes_n - 1, 1)),
    )


def _lap_halo(c, xm, xp, ylo, yhi, zlo, zhi, geo):
    rows, lanes, r_src, l_src = geo
    rows_n, lanes_n = c.shape
    (r1, r2), (l1, l2) = _rolled(c)
    y_out = jnp.where(rows == 0, ylo, yhi)
    z_out = jnp.where(lanes == 0, zlo, zhi)
    t1 = jnp.where(jnp.abs(r_src[0] - rows) == 1, r1, y_out)
    t2 = jnp.where(jnp.abs(r_src[1] - rows) == 1, r2, y_out)
    u1 = jnp.where(jnp.abs(l_src[0] - lanes) == 1, l1, z_out)
    u2 = jnp.where(jnp.abs(l_src[1] - lanes) == 1, l2, z_out)
    return (xp + xm) + (t1 + t2) + (u1 + u2) - 6.0 * c


def _lap_block(c, partner_x, geo):
    rows, lanes, r_src, l_src = geo
    (r1, r2), (l1, l2) = _rolled(c)
    t1 = jnp.where(r_src[0] // BY == rows // BY, r1, 0.0)
    t2 = jnp.where(r_src[1] // BY == rows // BY, r2, 0.0)
    u1 = jnp.where(l_src[0] // BZ == lanes // BZ, l1, 0.0)
    u2 = jnp.where(l_src[1] // BZ == lanes // BZ, l2, 0.0)
    return partner_x + (t1 + t2) + (u1 + u2) - 6.0 * c


def _couple(c_ref, vals, transpose):
    out = []
    for f in range(len(vals)):
        def m(g):
            return c_ref[g, f] if transpose else c_ref[f, g]
        acc = m(0) * vals[0]
        for g in range(1, len(vals)):
            acc = acc + m(g) * vals[g]
        out.append(acc)
    return out


def primal_kernel(c_ref, s_ref, d_ref, xlo, xhi, ylo, yhi, zlo, zhi,
                  s1_ref, eff_ref, oxlo, oxhi, oylo, oyhi, ozlo, ozhi):
    nf, nx, ny, nz = s_ref.shape
    geo = _masks(ny, nz)
    f32 = jnp.float32
    s = [[s_ref[f, x].astype(f32) for x in range(nx)] for f in range(nf)]
    for x in range(nx):
        d = d_ref[x].astype(f32)
        col = [s[f][x] for f in range(nf)]
        cs = _couple(c_ref, col, False)
        s1 = []
        for f in range(nf):
            xm = s[f][x - 1] if x > 0 else xlo[f, 0].astype(f32)
            xp = s[f][x + 1] if x < nx - 1 else xhi[f, 0].astype(f32)
            lap = _lap_halo(s[f][x], xm, xp, ylo[f, x].astype(f32), yhi[f, x].astype(f32),
                            zlo[f, x].astype(f32), zhi[f, x].astype(f32), geo)
            v = s[f][x] + primal_step * (d * lap + cs[f])
            s1.append(v)
            s1_ref[f, x] = v
            low = v.astype(jnp.bfloat16)
            if x == 0:
                oxlo[f, 0] = low
            if x == nx - 1:
                oxhi[f, 0] = low
            oylo[f, x] = low[0:1, :]
            oyhi[f, x] = low[ny - 1:ny, :]
            ozlo[f, x] = low[:, 0:1]
            ozhi[f, x] = low[:, nz - 1:nz]
        eff_ref[x] = (d * (1.0 + 0.5 * jnp.tanh(s1[0]))).astype(jnp.bfloat16)


def faces_kernel(s_ref, oxlo, oxhi, oylo, oyhi, ozlo, ozhi):
    nf, nx, ny, nz = s_ref.shape
    for f in range(nf):
        for x in range(nx):
            v = s_ref[f, x]
            if x == 0:
                oxlo[f, 0] = v
            if x == nx - 1:
                oxhi[f, 0] = v
            oylo[f, x] = v[0:1, :]
            oyhi[f, x] = v[ny - 1:ny, :]
            ozlo[f, x] = v[:, 0:1]
            ozhi[f, x] = v[:, nz - 1:nz]


def adjoint_kernel(c_ref, slot_ref, s1_ref, s_ref, d_ref, xlo, xhi, ylo, yhi, zlo, zhi, eff_ref, arr_ref,
                   w_ref, enr_ref, part_ref, spread_ref, goal_ref, react_ref):
    nf, nx, ny, nz = s_ref.shape
    geo = _masks(ny, nz)
    f32 = jnp.float32
    s1 = [[s1_ref[f, x] for x in range(nx)] for f in range(nf)]
    residual = [[None] * nx for _ in range(nf)]
    for x in range(nx):
        d = d_ref[x].astype(f32)
        cs = _couple(c_ref, [s1[f][x] for f in range(nf)], False)
        for f in range(nf):
            xm = s1[f][x - 1] if x > 0 else xlo[f, 0].astype(f32)
            xp = s1[f][x + 1] if x < nx - 1 else xhi[f, 0].astype(f32)
            lap = _lap_halo(s1[f][x], xm, xp, ylo[f, x].astype(f32), yhi[f, x].astype(f32),
                            zlo[f, x].astype(f32), zhi[f, x].astype(f32), geo)
            residual[f][x] = d * lap + cs[f] - (s1[f][x] - s_ref[f, x].astype(f32)) / primal_step
    for b in range(NBX * NBY * NBZ):
        bx, by, bz = b // (NBY * NBZ), (b // NBZ) % NBY, b % NBZ
        rows = arr_ref[slot_ref[b]].astype(f32)
        lanes = pl.ds(bz * BZ, BZ)
        for f in range(nf):
            rate = jnp.broadcast_to(rows[nf * BX * BY:nf * BX * BY + 1, f:f + 1], (1, BZ))
            for i in range(BX):
                for j in range(BY):
                    r = (f * BX + i) * BY + j
                    y = pl.ds(by * BY + j, 1)
                    goal_ref[f, bx * BX + i, y, lanes] = rows[r:r + 1, :]
                    react_ref[f, bx * BX + i, y, lanes] = rate
    eff = [eff_ref[x].astype(f32) for x in range(nx)]
    goal = [[goal_ref[f, x] for x in range(nx)] for f in range(nf)]
    react = [[react_ref[f, x] for x in range(nx)] for f in range(nf)]
    dual = [list(row) for row in goal]
    for _ in range(SECTIONS):
        new = [[None] * nx for _ in range(nf)]
        for x in range(nx):
            ct = _couple(c_ref, [dual[f][x] for f in range(nf)], True)
            for f in range(nf):
                lap = _lap_block(dual[f][x], dual[f][x ^ 1], geo)
                new[f][x] = dual[f][x] + dual_step * (
                    eff[x] * lap + ct[f] - react[f][x] * dual[f][x] + goal[f][x]
                )
        dual = new
    for bx in range(nx // BX):
        acc = None
        for x in range(bx * BX, bx * BX + BX):
            for f in range(nf):
                lap = _lap_block(dual[f][x], dual[f][x ^ 1], geo)
                e = (dual[f][x] + 0.125 * lap).astype(jnp.bfloat16)
                enr_ref[f, x] = e
                term = jnp.abs(residual[f][x] * e.astype(f32))
                acc = term if acc is None else acc + term
        part_ref[bx] = acc
        weighted = acc * w_ref[bx]
        total = weighted if bx == 0 else total + weighted
    total = jnp.sum(jnp.sum(total, axis=1, keepdims=True), axis=0, keepdims=True)
    spread_ref[...] = jnp.broadcast_to(total, spread_ref.shape)


def shards(state, diffusivity, coupling, owner, levels, mark_count, goal_weight, reaction):
    sides = (("gx", 1), ("gy", 2), ("gz", 3))
    dims = (1, 2, 3)

    slots = goal_weight.shape[0]
    packed = jnp.concatenate(
        [
            goal_weight.reshape(slots, FIELDS * BX * BY, BZ),
            jnp.pad(reaction, ((0, 0), (0, BZ - FIELDS)))[:, None, :],
        ],
        axis=1,
    )

    f32, bf16 = jnp.float32, jnp.bfloat16
    nf, nx, ny, nz = state.shape
    vmem = pl.BlockSpec(memory_space=pltpu.VMEM)
    smem = pl.BlockSpec(memory_space=pltpu.SMEM)
    face_shapes = [(nf, 1, ny, nz)] * 2 + [(nf, nx, 1, nz)] * 2 + [(nf, nx, ny, 1)] * 2
    state_faces = pl.pallas_call(
        faces_kernel,
        out_shape=[jax.ShapeDtypeStruct(shape, state.dtype) for shape in face_shapes],
        in_specs=[vmem],
        out_specs=[vmem] * 6,
    )(state)
    state_halo = []
    for (axis, _), low, high in zip(sides, state_faces[0::2], state_faces[1::2]):
        ends = lax.axis_size(axis) - 1
        state_halo.append(lax.ppermute(high, axis, [(i, i + 1) for i in range(ends)]))
        state_halo.append(lax.ppermute(low, axis, [(i + 1, i) for i in range(ends)]))
    packed, *state_halo = lax.optimization_barrier((packed, *state_halo))
    arrived = lax.all_to_all(packed, ("gy", "gz"), 0, 0, tiled=True)
    primal = pl.pallas_call(
        primal_kernel,
        out_shape=[jax.ShapeDtypeStruct(state.shape, f32), jax.ShapeDtypeStruct((nx, ny, nz), bf16)]
        + [jax.ShapeDtypeStruct(shape, bf16) for shape in face_shapes],
        in_specs=[smem] + [vmem] * 8,
        out_specs=[vmem] * 8,
    )(coupling, state, diffusivity, *state_halo)
    section_one, effective = primal[0], primal[1]
    section_halo = []
    for (axis, _), low, high in zip(sides, primal[2::2], primal[3::2]):
        ends = lax.axis_size(axis) - 1
        section_halo.append(lax.ppermute(high, axis, [(i, i + 1) for i in range(ends)]))
        section_halo.append(lax.ppermute(low, axis, [(i + 1, i) for i in range(ends)]))

    targets = owner[:, 0]
    order = jnp.arange(targets.shape[0], dtype=jnp.int32)
    same = targets[:, None] == targets[None, :]
    before = order[None, :] < order[:, None]
    rank = jnp.sum((same & before).astype(jnp.int32), axis=1)
    capacity = goal_weight.shape[0] // (lax.axis_size("gy") * lax.axis_size("gz"))
    slot_of = targets * capacity + rank

    weights = jnp.exp2(2.0 * levels.astype(jnp.float32))
    weight_cells = jnp.broadcast_to(
        weights.reshape(NBX, NBY, 1, NBZ, 1), (NBX, NBY, BY, NBZ, BZ)
    ).reshape(nx // BX, ny, nz)
    plane = lax.axis_size("gy") * lax.axis_size("gz")
    enriched, part, spread = pl.pallas_call(
        adjoint_kernel,
        out_shape=[
            jax.ShapeDtypeStruct(state.shape, bf16),
            jax.ShapeDtypeStruct((nx // BX, ny, nz), f32),
            jax.ShapeDtypeStruct((plane, 1), f32),
        ],
        in_specs=[smem, smem] + [vmem] * 12,
        out_specs=[vmem] * 3,
        scratch_shapes=[pltpu.VMEM(state.shape, f32), pltpu.VMEM(state.shape, f32)],
    )(coupling, slot_of, section_one, state, diffusivity, *section_halo, effective, arrived, weight_cells)
    sums = jnp.sum(part.reshape(nx // BX, ny // BY, BY, nz // BZ, BZ), axis=(2, 4)).reshape(-1)
    indicator = weights * sums

    across = lax.axis_size("gx")
    level_one = lax.all_to_all(spread, ("gy", "gz"), 0, 0, tiled=True)
    level_two = lax.all_to_all(
        jnp.broadcast_to(level_one.reshape(1, plane), (across, plane)), ("gx",), 0, 0, tiled=True
    )
    overall = jnp.sum(level_two)
    block_count = owner.shape[0] * lax.axis_size("gx") * lax.axis_size("gy") * lax.axis_size("gz")
    share = indicator * block_count / overall
    marked = jnp.minimum(1.0, mark_count[0].astype(jnp.float32) * indicator / overall)
    return (enriched, share, marked)


def solution(mesh):
    placed = (
        P(None, "gx", "gy", "gz"),
        P("gx", "gy", "gz"),
        P(),
        P(("gx", "gy", "gz"), None),
        P(("gx", "gy", "gz")),
        P(),
        P(("gx", "gy", "gz"), None, None, None, None),
        P(("gx", "gy", "gz"), None),
    )
    return jax.shard_map(
        shards,
        mesh=mesh,
        in_specs=placed,
        out_specs=(P(None, "gx", "gy", "gz"), P(("gx", "gy", "gz")), P(("gx", "gy", "gz"))),
        check_vma=False,
    )
```

```python
import jax
import jax.numpy as jnp
from jax import lax
from jax.experimental import pallas as pl
from jax.experimental.pallas import tpu as pltpu
from jax.sharding import PartitionSpec as P

BX = 2
BY = 2
BZ = 128
NBX = 2
NBY = 4
NBZ = 6
SECTIONS = 3
FIELDS = 5


primal_step = 0.05
dual_step = 0.05

REDUCE = "exchange"


def faces(cells, sides):
    out = []
    for axis, dim in sides:
        count = lax.axis_size(axis)
        ends = count - 1
        head = lax.slice_in_dim(cells, 0, 1, axis=dim)
        tail = lax.slice_in_dim(cells, cells.shape[dim] - 1, cells.shape[dim], axis=dim)
        below = lax.ppermute(tail, axis, [(i, i + 1) for i in range(ends)])
        above = lax.ppermute(head, axis, [(i + 1, i) for i in range(ends)])
        out.append((below, above))
    return out


def shifted(v, dim, below, above):
    n = v.shape[dim]
    minus = jnp.concatenate([below, lax.slice_in_dim(v, 0, n - 1, axis=dim)], axis=dim)
    plus = jnp.concatenate([lax.slice_in_dim(v, 1, n, axis=dim), above], axis=dim)
    return minus, plus


def laplace_halo(v, halos, dims):
    total = None
    for (below, above), dim in zip(halos, dims):
        minus, plus = shifted(v, dim, below.astype(v.dtype), above.astype(v.dtype))
        pair = minus + plus
        total = pair if total is None else total + pair
    return total - 6.0 * v


def block_shift(v, dim, width):
    n = v.shape[dim]
    zero = jnp.zeros_like(lax.slice_in_dim(v, 0, 1, axis=dim))
    minus = jnp.concatenate([zero, lax.slice_in_dim(v, 0, n - 1, axis=dim)], axis=dim)
    plus = jnp.concatenate([lax.slice_in_dim(v, 1, n, axis=dim), zero], axis=dim)
    pos = lax.broadcasted_iota(jnp.int32, v.shape, dim) % width
    minus = jnp.where(pos == 0, 0.0, minus)
    plus = jnp.where(pos == width - 1, 0.0, plus)
    return minus + plus


def laplace_blocks(v):
    return block_shift(v, 1, BX) + block_shift(v, 2, BY) + block_shift(v, 3, BZ) - 6.0 * v


def couple(matrix, v):
    return jnp.sum(matrix[:, :, None, None, None] * v[None], axis=1)


def global_sum(x):
    if REDUCE == "psum":
        return lax.psum(x, ("gx", "gy", "gz"))
    if REDUCE == "exchange":
        for group in (("gy", "gz"), ("gx",)):
            count = 1
            for axis in group:
                count *= lax.axis_size(axis)
            spread = jnp.broadcast_to(x.reshape(1), (count,))
            x = jnp.sum(lax.all_to_all(spread, group, 0, 0, tiled=True))
        return x
    if REDUCE == "gather":
        every = lax.all_gather(x.reshape(1), ("gx", "gy", "gz"), tiled=True)
        return jnp.sum(every)
    for axis in ("gz", "gy", "gx"):
        n = lax.axis_size(axis)
        step = 1
        while step < n:
            x = x + lax.ppermute(x, axis, [(i, (i + step) % n) for i in range(n)])
            step *= 2
    return x


def to_cells(blocks):
    depth = blocks.shape[1]
    shaped = blocks.reshape(NBX, NBY, NBZ, depth, BX, BY, BZ)
    return shaped.transpose(3, 0, 4, 1, 5, 2, 6).reshape(depth, NBX * BX, NBY * BY, NBZ * BZ)


def per_block_cells(values):
    depth = values.shape[1]
    shaped = values.reshape(NBX, NBY, NBZ, depth).transpose(3, 0, 1, 2)
    shaped = jnp.broadcast_to(
        shaped[:, :, None, :, None, :, None], (depth, NBX, BX, NBY, BY, NBZ, BZ)
    )
    return shaped.reshape(depth, NBX * BX, NBY * BY, NBZ * BZ)


def block_sums(cells):
    depth = cells.shape[0]
    shaped = cells.reshape(depth, NBX, BX, NBY, BY, NBZ, BZ)
    return jnp.sum(shaped, axis=(0, 2, 4, 6)).reshape(NBX * NBY * NBZ)


def _masks(rows_n, lanes_n):
    rows = lax.broadcasted_iota(jnp.int32, (rows_n, lanes_n), 0)
    lanes = lax.broadcasted_iota(jnp.int32, (rows_n, lanes_n), 1)
    r_src = (pltpu.roll(rows, 1, 0), pltpu.roll(rows, rows_n - 1, 0))
    l_src = (pltpu.roll(lanes, 1, 1), pltpu.roll(lanes, lanes_n - 1, 1))
    return rows, lanes, r_src, l_src


def _rolled(v):
    rows_n, lanes_n = v.shape
    return (
        (pltpu.roll(v, 1, 0), pltpu.roll(v, rows_n - 1, 0)),
        (pltpu.roll(v, 1, 1), pltpu.roll(v, lanes_n - 1, 1)),
    )


def _lap_halo(c, xm, xp, ylo, yhi, zlo, zhi, geo):
    rows, lanes, r_src, l_src = geo
    rows_n, lanes_n = c.shape
    (r1, r2), (l1, l2) = _rolled(c)
    y_out = jnp.where(rows == 0, ylo, yhi)
    z_out = jnp.where(lanes == 0, zlo, zhi)
    t1 = jnp.where(jnp.abs(r_src[0] - rows) == 1, r1, y_out)
    t2 = jnp.where(jnp.abs(r_src[1] - rows) == 1, r2, y_out)
    u1 = jnp.where(jnp.abs(l_src[0] - lanes) == 1, l1, z_out)
    u2 = jnp.where(jnp.abs(l_src[1] - lanes) == 1, l2, z_out)
    return (xp + xm) + (t1 + t2) + (u1 + u2) - 6.0 * c


def _lap_block(c, partner_x, geo):
    rows, lanes, r_src, l_src = geo
    (r1, r2), (l1, l2) = _rolled(c)
    t1 = jnp.where(r_src[0] // BY == rows // BY, r1, 0.0)
    t2 = jnp.where(r_src[1] // BY == rows // BY, r2, 0.0)
    u1 = jnp.where(l_src[0] // BZ == lanes // BZ, l1, 0.0)
    u2 = jnp.where(l_src[1] // BZ == lanes // BZ, l2, 0.0)
    return partner_x + (t1 + t2) + (u1 + u2) - 6.0 * c


def _couple(c_ref, vals, transpose):
    out = []
    for f in range(len(vals)):
        def m(g):
            return c_ref[g, f] if transpose else c_ref[f, g]
        acc = m(0) * vals[0]
        for g in range(1, len(vals)):
            acc = acc + m(g) * vals[g]
        out.append(acc)
    return out


def primal_kernel(c_ref, s_ref, d_ref, xlo, xhi, ylo, yhi, zlo, zhi,
                  s1_ref, eff_ref, oxlo, oxhi, oylo, oyhi, ozlo, ozhi):
    nf, nx, ny, nz = s_ref.shape
    geo = _masks(ny, nz)
    f32 = jnp.float32
    s = [[s_ref[f, x].astype(f32) for x in range(nx)] for f in range(nf)]
    for x in range(nx):
        d = d_ref[x].astype(f32)
        col = [s[f][x] for f in range(nf)]
        cs = _couple(c_ref, col, False)
        s1 = []
        for f in range(nf):
            xm = s[f][x - 1] if x > 0 else xlo[f, 0].astype(f32)
            xp = s[f][x + 1] if x < nx - 1 else xhi[f, 0].astype(f32)
            lap = _lap_halo(s[f][x], xm, xp, ylo[f, x].astype(f32), yhi[f, x].astype(f32),
                            zlo[f, x].astype(f32), zhi[f, x].astype(f32), geo)
            v = s[f][x] + primal_step * (d * lap + cs[f])
            s1.append(v)
            s1_ref[f, x] = v
            low = v.astype(jnp.bfloat16)
            if x == 0:
                oxlo[f, 0] = low
            if x == nx - 1:
                oxhi[f, 0] = low
            oylo[f, x] = low[0:1, :]
            oyhi[f, x] = low[ny - 1:ny, :]
            ozlo[f, x] = low[:, 0:1]
            ozhi[f, x] = low[:, nz - 1:nz]
        eff_ref[x] = (d * (1.0 + 0.5 * jnp.tanh(s1[0]))).astype(jnp.bfloat16)


def faces_kernel(s_ref, oxlo, oxhi, oylo, oyhi, ozlo, ozhi):
    nf, nx, ny, nz = s_ref.shape
    for f in range(nf):
        for x in range(nx):
            v = s_ref[f, x]
            if x == 0:
                oxlo[f, 0] = v
            if x == nx - 1:
                oxhi[f, 0] = v
            oylo[f, x] = v[0:1, :]
            oyhi[f, x] = v[ny - 1:ny, :]
            ozlo[f, x] = v[:, 0:1]
            ozhi[f, x] = v[:, nz - 1:nz]


def adjoint_kernel(c_ref, slot_ref, s1_ref, s_ref, d_ref, xlo, xhi, ylo, yhi, zlo, zhi, eff_ref, arr_ref,
                   w_ref, enr_ref, part_ref, spread_ref, goal_ref, react_ref):
    nf, nx, ny, nz = s_ref.shape
    geo = _masks(ny, nz)
    f32 = jnp.float32
    s1 = [[s1_ref[f, x] for x in range(nx)] for f in range(nf)]
    residual = [[None] * nx for _ in range(nf)]
    for x in range(nx):
        d = d_ref[x].astype(f32)
        cs = _couple(c_ref, [s1[f][x] for f in range(nf)], False)
        for f in range(nf):
            xm = s1[f][x - 1] if x > 0 else xlo[f, 0].astype(f32)
            xp = s1[f][x + 1] if x < nx - 1 else xhi[f, 0].astype(f32)
            lap = _lap_halo(s1[f][x], xm, xp, ylo[f, x].astype(f32), yhi[f, x].astype(f32),
                            zlo[f, x].astype(f32), zhi[f, x].astype(f32), geo)
            residual[f][x] = d * lap + cs[f] - (s1[f][x] - s_ref[f, x].astype(f32)) / primal_step
    for b in range(NBX * NBY * NBZ):
        bx, by, bz = b // (NBY * NBZ), (b // NBZ) % NBY, b % NBZ
        rows = arr_ref[slot_ref[b]].astype(f32)
        lanes = pl.ds(bz * BZ, BZ)
        for f in range(nf):
            rate = jnp.broadcast_to(rows[nf * BX * BY:nf * BX * BY + 1, f:f + 1], (1, BZ))
            for i in range(BX):
                for j in range(BY):
                    r = (f * BX + i) * BY + j
                    y = pl.ds(by * BY + j, 1)
                    goal_ref[f, bx * BX + i, y, lanes] = rows[r:r + 1, :]
                    react_ref[f, bx * BX + i, y, lanes] = rate
    eff = [eff_ref[x].astype(f32) for x in range(nx)]
    goal = [[goal_ref[f, x] for x in range(nx)] for f in range(nf)]
    react = [[react_ref[f, x] for x in range(nx)] for f in range(nf)]
    dual = [list(row) for row in goal]
    for _ in range(SECTIONS):
        new = [[None] * nx for _ in range(nf)]
        for x in range(nx):
            ct = _couple(c_ref, [dual[f][x] for f in range(nf)], True)
            for f in range(nf):
                lap = _lap_block(dual[f][x], dual[f][x ^ 1], geo)
                new[f][x] = dual[f][x] + dual_step * (
                    eff[x] * lap + ct[f] - react[f][x] * dual[f][x] + goal[f][x]
                )
        dual = new
    for bx in range(nx // BX):
        acc = None
        for x in range(bx * BX, bx * BX + BX):
            for f in range(nf):
                lap = _lap_block(dual[f][x], dual[f][x ^ 1], geo)
                e = (dual[f][x] + 0.125 * lap).astype(jnp.bfloat16)
                enr_ref[f, x] = e
                term = jnp.abs(residual[f][x] * e.astype(f32))
                acc = term if acc is None else acc + term
        part_ref[bx] = acc
        weighted = acc * w_ref[bx]
        total = weighted if bx == 0 else total + weighted
    total = jnp.sum(jnp.sum(total, axis=1, keepdims=True), axis=0, keepdims=True)
    spread_ref[...] = jnp.broadcast_to(total, spread_ref.shape)


def shards(state, diffusivity, coupling, owner, levels, mark_count, goal_weight, reaction):
    sides = (("gx", 1), ("gy", 2), ("gz", 3))
    dims = (1, 2, 3)

    slots = goal_weight.shape[0]
    packed = jnp.concatenate(
        [
            goal_weight.reshape(slots, FIELDS * BX * BY, BZ),
            jnp.pad(reaction, ((0, 0), (0, BZ - FIELDS)))[:, None, :],
        ],
        axis=1,
    )

    f32, bf16 = jnp.float32, jnp.bfloat16
    nf, nx, ny, nz = state.shape
    vmem = pl.BlockSpec(memory_space=pltpu.VMEM)
    smem = pl.BlockSpec(memory_space=pltpu.SMEM)
    face_shapes = [(nf, 1, ny, nz)] * 2 + [(nf, nx, 1, nz)] * 2 + [(nf, nx, ny, 1)] * 2
    state_faces = pl.pallas_call(
        faces_kernel,
        out_shape=[jax.ShapeDtypeStruct(shape, state.dtype) for shape in face_shapes],
        in_specs=[vmem],
        out_specs=[vmem] * 6,
    )(state)
    state_halo = []
    for (axis, _), low, high in zip(sides, state_faces[0::2], state_faces[1::2]):
        ends = lax.axis_size(axis) - 1
        state_halo.append(lax.ppermute(high, axis, [(i, i + 1) for i in range(ends)]))
        state_halo.append(lax.ppermute(low, axis, [(i + 1, i) for i in range(ends)]))
    arrived = lax.all_to_all(packed, ("gy", "gz"), 0, 0, tiled=True)
    primal = pl.pallas_call(
        primal_kernel,
        out_shape=[jax.ShapeDtypeStruct(state.shape, f32), jax.ShapeDtypeStruct((nx, ny, nz), bf16)]
        + [jax.ShapeDtypeStruct(shape, bf16) for shape in face_shapes],
        in_specs=[smem] + [vmem] * 8,
        out_specs=[vmem] * 8,
    )(coupling, state, diffusivity, *state_halo)
    section_one, effective = primal[0], primal[1]
    section_halo = []
    for (axis, _), low, high in zip(sides, primal[2::2], primal[3::2]):
        ends = lax.axis_size(axis) - 1
        section_halo.append(lax.ppermute(high, axis, [(i, i + 1) for i in range(ends)]))
        section_halo.append(lax.ppermute(low, axis, [(i + 1, i) for i in range(ends)]))

    targets = owner[:, 0]
    order = jnp.arange(targets.shape[0], dtype=jnp.int32)
    same = targets[:, None] == targets[None, :]
    before = order[None, :] < order[:, None]
    rank = jnp.sum((same & before).astype(jnp.int32), axis=1)
    capacity = goal_weight.shape[0] // (lax.axis_size("gy") * lax.axis_size("gz"))
    slot_of = targets * capacity + rank

    weights = jnp.exp2(2.0 * levels.astype(jnp.float32))
    weight_cells = jnp.broadcast_to(
        weights.reshape(NBX, NBY, 1, NBZ, 1), (NBX, NBY, BY, NBZ, BZ)
    ).reshape(nx // BX, ny, nz)
    plane = lax.axis_size("gy") * lax.axis_size("gz")
    enriched, part, spread = pl.pallas_call(
        adjoint_kernel,
        out_shape=[
            jax.ShapeDtypeStruct(state.shape, bf16),
            jax.ShapeDtypeStruct((nx // BX, ny, nz), f32),
            jax.ShapeDtypeStruct((plane, 1), f32),
        ],
        in_specs=[smem, smem] + [vmem] * 12,
        out_specs=[vmem] * 3,
        scratch_shapes=[pltpu.VMEM(state.shape, f32), pltpu.VMEM(state.shape, f32)],
    )(coupling, slot_of, section_one, state, diffusivity, *section_halo, effective, arrived, weight_cells)
    sums = jnp.sum(part.reshape(nx // BX, ny // BY, BY, nz // BZ, BZ), axis=(2, 4)).reshape(-1)
    indicator = weights * sums

    across = lax.axis_size("gx")
    level_one = lax.all_to_all(spread, ("gy", "gz"), 0, 0, tiled=True)
    level_two = lax.all_to_all(
        jnp.broadcast_to(level_one.reshape(1, plane), (across, plane)), ("gx",), 0, 0, tiled=True
    )
    overall = jnp.sum(level_two)
    block_count = owner.shape[0] * lax.axis_size("gx") * lax.axis_size("gy") * lax.axis_size("gz")
    share = indicator * block_count / overall
    marked = jnp.minimum(1.0, mark_count[0].astype(jnp.float32) * indicator / overall)
    return (enriched, share, marked)


def solution(mesh):
    placed = (
        P(None, "gx", "gy", "gz"),
        P("gx", "gy", "gz"),
        P(),
        P(("gx", "gy", "gz"), None),
        P(("gx", "gy", "gz")),
        P(),
        P(("gx", "gy", "gz"), None, None, None, None),
        P(("gx", "gy", "gz"), None),
    )
    return jax.shard_map(
        shards,
        mesh=mesh,
        in_specs=placed,
        out_specs=(P(None, "gx", "gy", "gz"), P(("gx", "gy", "gz")), P(("gx", "gy", "gz"))),
        check_vma=False,
    )
```
